256 devices in a mesh: chan: 64 (over y, z_lo, x), win: 4 (over z_hi, core).
Axes of the slice: x: 4, y: 4, z: 8 (z_hi: 2, z_lo: 4; z = z_hi * 4 + z_lo), core: 2. Of those that a mesh axis runs over, the one named last changes fastest.
Arguments:
- records: bfloat16 [4, 1024, 7680], P('win', 'chan'), may hold values from -6 to 6
- source_rows: int32 [1, 256], replicated, may hold values from 0 to 15
Outputs:
- correlation: float32 [256, 1024, 2048], P(None, ('chan', 'win'))
The draws below stay inside these ranges and needn't reach their ends.
Inputs may be any that keep to these rules, and one draw needn't show every extreme that they name: Entry j of row b of source_rows names a channel of channel shard j // 4, counted within that shard; entries may repeat.
All inputs are finite; a program needn't handle non-finite values.
Results may differ from the reference program's by a relative error of at most 0.0063.
Values may be sent and summed in bfloat16 or wider, within the bound.
No kernel may reach another device: no remote copies, remote signals or barrier semaphores. Data moves between devices by JAX's collectives and lax.ppermute only.
A program may use at most 64 MiB of HBM per device.

```python
import math
import jax
import jax.numpy as jnp
from jax import lax

S = 7680
NBINS = 512
HALF = 32
FIRST_BIN = 64
MAXLAG = 1024
BLOCK = 256
R_DEV = 16
STEPS = 1
CHANNELS = 1024
WINDOWS = 4
SOURCES = 256
N_CHAN = 64


def with_ends(values, own_key, least, top_value):
    place = [jax.random.randint(jax.random.fold_in(own_key, axis), (), 0, length) for axis, length in enumerate(values.shape)]
    widest = values.shape.index(max(values.shape))
    neighbour = place[:widest] + [(place[widest] + 1) % values.shape[widest]] + place[widest + 1:]
    return values.at[tuple(place)].set(least).at[tuple(neighbour)].set(top_value)


def level_of(own_key, dims, split, low, top_value):
    gain = 1.0
    for position, shards_of in split:
        steps = jax.random.uniform(jax.random.fold_in(jax.random.fold_in(own_key, 6), position), (shards_of,), jnp.float32, low / len(split), top_value / len(split))
        gain = gain * jnp.repeat(jnp.exp(steps), dims[position] // shards_of).reshape((-1,) + (1,) * (len(dims) - 1 - position))
    return gain


def noise(stream_key, shape, spread, reach, shards=(), held_as=jnp.bfloat16):
    values = spread * jax.random.normal(stream_key, shape, jnp.float32)
    if shards:
        values = values * level_of(stream_key, shape, shards, -0.22, 0.18)
    return jnp.clip(values, -reach, reach).astype(held_as)


def setup_inputs(seed: int = 0) -> dict:
    arg_keys = jax.random.split(jax.random.key(seed), 3)
    records = noise(arg_keys[0], (WINDOWS, CHANNELS, S), 1.0, 6.0, ((0, 4), (1, 64)))
    source_rows = with_ends(jax.random.randint(arg_keys[1], (STEPS, BLOCK), 0, R_DEV), jax.random.fold_in(arg_keys[1], 1), 0, R_DEV - 1).astype(jnp.int32)
    return dict(records=records, source_rows=source_rows)


full_turn = 2.0 * math.pi

def band_table():
    bin_ids = FIRST_BIN - HALF + jnp.arange(NBINS + 2 * HALF, dtype=jnp.int32)
    sample_ids = jnp.arange(S, dtype=jnp.int32)
    angles = (sample_ids[:, None] * bin_ids[None, :] % S).astype(jnp.float32) * (full_turn / S)
    return jnp.concatenate([jnp.cos(angles), -jnp.sin(angles)], axis=1).astype(jnp.bfloat16)

def lag_weights():
    bin_ids = FIRST_BIN + jnp.arange(NBINS, dtype=jnp.int32)
    lag_ids = jnp.arange(2 * MAXLAG, dtype=jnp.int32) - MAXLAG
    angles = (bin_ids[:, None] * lag_ids[None, :] % S).astype(jnp.float32) * (full_turn / S)
    return jnp.concatenate([jnp.cos(angles), -jnp.sin(angles)], axis=0).astype(jnp.bfloat16)

def normalize(spectrum):
    extent = NBINS + 2 * HALF
    real_part = spectrum[:, :extent]
    imag_part = spectrum[:, extent:]
    magnitude = jnp.sqrt(real_part * real_part + imag_part * imag_part)
    smooth = magnitude[:, 0:NBINS]
    for offset in range(1, 2 * HALF + 1):
        smooth = smooth + magnitude[:, offset:offset + NBINS]
    smooth = smooth / (2 * HALF + 1) + 1e-06
    centre_re = real_part[:, HALF:HALF + NBINS] / smooth
    centre_im = imag_part[:, HALF:HALF + NBINS] / smooth
    return jnp.stack([centre_re, centre_im], axis=1).astype(jnp.bfloat16)

def cross_terms(source_part, receiver_part):
    first = source_part.astype(jnp.float32)
    second = receiver_part.astype(jnp.float32)
    real_sum = jnp.einsum('wbi,wri->bri', first[:, :, 0], second[:, :, 0]) + jnp.einsum('wbi,wri->bri', first[:, :, 1], second[:, :, 1])
    imag_sum = jnp.einsum('wbi,wri->bri', first[:, :, 1], second[:, :, 0]) - jnp.einsum('wbi,wri->bri', first[:, :, 0], second[:, :, 1])
    return jnp.stack([real_sum, imag_sum], axis=2)

def reference(records, source_rows):
    flat = records.reshape(WINDOWS * CHANNELS, S)
    whitened = normalize(jnp.dot(flat, band_table(), preferred_element_type=jnp.float32))
    whitened = whitened.reshape(WINDOWS, CHANNELS, 2, NBINS)
    per_shard = BLOCK // N_CHAN
    base_rows = jnp.arange(BLOCK, dtype=jnp.int32) // per_shard * R_DEV
    source_index = (base_rows[None, :] + source_rows).astype(jnp.int32)
    picked = jnp.take(whitened, source_index.reshape(-1), axis=1)
    grouped = picked.reshape(WINDOWS, SOURCES // 8, 8, 2, NBINS).transpose(1, 0, 2, 3, 4)
    weights = lag_weights()
    lag_scale = math.sqrt(2.0 / (WINDOWS * NBINS))

    def per_group(member):
        spectra = cross_terms(member, whitened)
        rounded = spectra.astype(jnp.bfloat16).reshape(8 * CHANNELS, 2 * NBINS)
        result = jnp.dot(rounded, weights, preferred_element_type=jnp.float32) * lag_scale
        return result.reshape(8, CHANNELS, 2 * MAXLAG)
    outcome = lax.map(per_group, grouped)
    return outcome.reshape(SOURCES, CHANNELS, 2 * MAXLAG)
```

```python
import math

import jax
import jax.numpy as jnp
from jax import lax
from jax.sharding import PartitionSpec as P

S = 7680
NBINS = 512
HALF = 32
FIRST_BIN = 64
MAXLAG = 1024


full_turn = 2.0 * math.pi


def band_table():
    bin_ids = FIRST_BIN - HALF + jnp.arange(NBINS + 2 * HALF, dtype=jnp.int32)
    sample_ids = jnp.arange(S, dtype=jnp.int32)
    angles = (sample_ids[:, None] * bin_ids[None, :] % S).astype(jnp.float32) * (full_turn / S)
    return jnp.concatenate([jnp.cos(angles), -jnp.sin(angles)], axis=1).astype(jnp.bfloat16)


def lag_weights():
    bin_ids = FIRST_BIN + jnp.arange(NBINS, dtype=jnp.int32)
    lag_ids = jnp.arange(2 * MAXLAG, dtype=jnp.int32) - MAXLAG
    angles = (bin_ids[:, None] * lag_ids[None, :] % S).astype(jnp.float32) * (full_turn / S)
    return jnp.concatenate([jnp.cos(angles), -jnp.sin(angles)], axis=0).astype(jnp.bfloat16)


def normalize(spectrum):
    extent = NBINS + 2 * HALF
    real_part = spectrum[:, :extent]
    imag_part = spectrum[:, extent:]
    magnitude = jnp.sqrt(real_part * real_part + imag_part * imag_part)
    smooth = magnitude[:, 0:NBINS]
    for offset in range(1, 2 * HALF + 1):
        smooth = smooth + magnitude[:, offset : offset + NBINS]
    smooth = smooth / (2 * HALF + 1) + 1e-06
    centre_re = real_part[:, HALF : HALF + NBINS] / smooth
    centre_im = imag_part[:, HALF : HALF + NBINS] / smooth
    return jnp.stack([centre_re, centre_im], axis=1).astype(jnp.bfloat16)


def whiten(row_data):
    return normalize(jnp.dot(row_data, band_table(), preferred_element_type=jnp.float32))


def cross_terms(source_part, receiver_part):
    real_sum = jnp.einsum(
        "wbi,wri->bri",
        source_part[:, :, 0],
        receiver_part[:, :, 0],
        preferred_element_type=jnp.float32,
    ) + jnp.einsum(
        "wbi,wri->bri",
        source_part[:, :, 1],
        receiver_part[:, :, 1],
        preferred_element_type=jnp.float32,
    )
    imag_sum = jnp.einsum(
        "wbi,wri->bri",
        source_part[:, :, 1],
        receiver_part[:, :, 0],
        preferred_element_type=jnp.float32,
    ) - jnp.einsum(
        "wbi,wri->bri",
        source_part[:, :, 0],
        receiver_part[:, :, 1],
        preferred_element_type=jnp.float32,
    )
    return jnp.stack([real_sum, imag_sum], axis=2)


def transform(spectra, weights, lag_scale):
    count_src, count_rec = (spectra.shape[0], spectra.shape[1])
    rounded = spectra.astype(jnp.bfloat16).reshape(count_src * count_rec, 2 * NBINS)
    result = jnp.dot(rounded, weights, preferred_element_type=jnp.float32) * lag_scale
    return result.reshape(count_src, count_rec, 2 * MAXLAG)


def collect(portion):
    portion = lax.all_gather(portion, "win", axis=0, tiled=True)
    return lax.all_gather(portion, "chan", axis=1, tiled=True)


def per_device(records, source_rows):
    windows_here, rows_here, samples = records.shape
    whitened = whiten(records.reshape(windows_here * rows_here, samples)).reshape(
        windows_here, rows_here, 2, NBINS
    )
    shards = lax.axis_size("chan")
    block_len = source_rows.shape[1]
    per_shard = block_len // shards
    weights = lag_weights()
    lag_scale = math.sqrt(2.0 / (lax.axis_size("win") * windows_here * NBINS))
    receivers = lax.all_to_all(whitened, "win", split_axis=1, concat_axis=0, tiled=True)
    shard = lax.axis_index("chan")
    own_rows = lax.dynamic_slice_in_dim(source_rows[0], shard * per_shard, per_shard)
    own_sources = jnp.take(whitened, own_rows, axis=1)
    source_block = collect(own_sources)
    spectra = cross_terms(source_block, receivers)
    results = transform(spectra, weights, lag_scale)
    return results


def solution(mesh):
    in_specs = (P("win", "chan", None), P())
    out_specs = P(None, ("chan", "win"), None)
    return jax.shard_map(
        per_device, mesh=mesh, in_specs=in_specs, out_specs=out_specs, check_vma=False
    )
```

```python
import math

import numpy as np

import jax
import jax.numpy as jnp
from jax import lax
from jax.sharding import Mesh, PartitionSpec as P

S = 7680
NBINS = 512
HALF = 32
FIRST_BIN = 64
MAXLAG = 1024

CHAN_AXES = ("y", "zl", "x")
WIN_AXES = ("zh", "core")


def angle_table(rows, cols):
    turns = np.mod(np.outer(rows.astype(np.int64), cols.astype(np.int64)), S).astype(np.float64)
    angles = turns * (2.0 * np.pi / S)
    return np.cos(angles).astype(np.float32), np.sin(angles).astype(np.float32)


def band_table():
    extent = NBINS + 2 * HALF
    bin_ids = np.arange(FIRST_BIN - HALF, FIRST_BIN - HALF + extent)
    inner = 128
    outer = S // inner
    cq, sq = angle_table(np.arange(outer) * inner, bin_ids)
    cr, sr = angle_table(np.arange(inner), bin_ids)
    cq, sq, cr, sr = (jnp.asarray(a) for a in (cq, sq, cr, sr))
    cos = cq[:, None, :] * cr[None, :, :] - sq[:, None, :] * sr[None, :, :]
    sin = sq[:, None, :] * cr[None, :, :] + cq[:, None, :] * sr[None, :, :]
    table = jnp.concatenate([cos, -sin], axis=2).astype(jnp.bfloat16)
    return table.reshape(S, 2 * extent)


def lag_weights():
    bin_ids = FIRST_BIN + np.arange(NBINS)
    inner = 64
    outer = 2 * MAXLAG // inner
    ca, sa = angle_table(bin_ids, (np.arange(outer) - MAXLAG // inner) * inner)
    cb, sb = angle_table(bin_ids, np.arange(inner))
    ca, sa, cb, sb = (jnp.asarray(a) for a in (ca, sa, cb, sb))
    cos = ca[:, :, None] * cb[:, None, :] - sa[:, :, None] * sb[:, None, :]
    sin = sa[:, :, None] * cb[:, None, :] + ca[:, :, None] * sb[:, None, :]
    table = jnp.concatenate([cos, -sin], axis=0).astype(jnp.bfloat16)
    return table.reshape(2 * NBINS, 2 * MAXLAG)


def normalize(spectrum):
    extent = NBINS + 2 * HALF
    real_part = spectrum[:, :extent]
    imag_part = spectrum[:, extent:]
    magnitude = jnp.sqrt(real_part * real_part + imag_part * imag_part)
    smooth = magnitude[:, 0:NBINS]
    for offset in range(1, 2 * HALF + 1):
        smooth = smooth + magnitude[:, offset : offset + NBINS]
    smooth = smooth / (2 * HALF + 1) + 1e-06
    centre_re = real_part[:, HALF : HALF + NBINS] / smooth
    centre_im = imag_part[:, HALF : HALF + NBINS] / smooth
    return jnp.stack([centre_re, centre_im], axis=1).astype(jnp.bfloat16)


def whiten(row_data):
    return normalize(jnp.dot(row_data, band_table(), preferred_element_type=jnp.float32))


def cross_terms(source_part, receiver_part):
    real_sum = jnp.einsum(
        "wbi,wri->bri",
        source_part[:, :, 0],
        receiver_part[:, :, 0],
        preferred_element_type=jnp.float32,
    ) + jnp.einsum(
        "wbi,wri->bri",
        source_part[:, :, 1],
        receiver_part[:, :, 1],
        preferred_element_type=jnp.float32,
    )
    imag_sum = jnp.einsum(
        "wbi,wri->bri",
        source_part[:, :, 1],
        receiver_part[:, :, 0],
        preferred_element_type=jnp.float32,
    ) - jnp.einsum(
        "wbi,wri->bri",
        source_part[:, :, 0],
        receiver_part[:, :, 1],
        preferred_element_type=jnp.float32,
    )
    return jnp.stack([real_sum, imag_sum], axis=2)


def transform(spectra, weights, lag_scale):
    count_src, count_rec = (spectra.shape[0], spectra.shape[1])
    rounded = spectra.astype(jnp.bfloat16).reshape(count_src * count_rec, 2 * NBINS)
    result = jnp.dot(rounded, weights, preferred_element_type=jnp.float32) * lag_scale
    return result.reshape(count_src, count_rec, 2 * MAXLAG)


def ring_gather(value, axis_name, axis):
    size = lax.axis_size(axis_name)
    here = lax.axis_index(axis_name)
    parts = [value] + [
        lax.ppermute(value, axis_name, [(i, (i + shift) % size) for i in range(size)])
        for shift in range(1, size)
    ]
    stacked = jnp.stack(parts, 0)
    stacked = jnp.take(stacked, (here - jnp.arange(size)) % size, axis=0)
    stacked = jnp.moveaxis(stacked, 0, axis)
    shape = list(value.shape)
    shape[axis] *= size
    return stacked.reshape(shape)


def collect(own):
    part = ring_gather(own[None], "zh", 0)
    for name in reversed(CHAN_AXES):
        part = ring_gather(part, name, 2)
    part = ring_gather(part[None], "core", 0)
    part = jnp.swapaxes(part, 0, 1)
    return part.reshape(-1, part.shape[3], 2, NBINS)


def per_device(records, source_rows):
    windows_here, rows_here, samples = records.shape
    whitened = whiten(records.reshape(windows_here * rows_here, samples)).reshape(
        windows_here, rows_here, 2, NBINS
    )
    shards = lax.axis_size(CHAN_AXES)
    block_len = source_rows.shape[1]
    per_shard = block_len // shards
    weights = lag_weights()
    lag_scale = math.sqrt(2.0 / (lax.axis_size(WIN_AXES) * windows_here * NBINS))
    receivers = lax.all_to_all(whitened, WIN_AXES, split_axis=1, concat_axis=0, tiled=True)
    shard = lax.axis_index(CHAN_AXES)
    own_rows = lax.dynamic_slice_in_dim(source_rows[0], shard * per_shard, per_shard)
    own_sources = jnp.take(whitened, own_rows, axis=1)
    source_block = collect(own_sources)
    spectra = cross_terms(source_block, receivers)
    results = transform(spectra, weights, lag_scale)
    return results


def split_mesh(mesh):
    chan, win = mesh.shape["chan"], mesh.shape["win"]
    side = round(chan ** (1 / 3))
    devices = np.asarray(mesh.devices).reshape(side, side, chan // (side * side), win // 2, 2)
    return Mesh(devices, CHAN_AXES + WIN_AXES)


def solution(mesh):
    fine = split_mesh(mesh)
    in_specs = (P(WIN_AXES, CHAN_AXES, None), P())
    out_specs = P(None, CHAN_AXES + WIN_AXES, None)
    return jax.shard_map(
        per_device, mesh=fine, in_specs=in_specs, out_specs=out_specs, check_vma=False
    )
```

```python
import math

import numpy as np

import jax
import jax.numpy as jnp
from jax import lax
from jax.sharding import Mesh, PartitionSpec as P

S = 7680
NBINS = 512
HALF = 32
FIRST_BIN = 64
MAXLAG = 1024

CHAN_AXES = ("y", "zl", "x")
WIN_AXES = ("zh", "core")


def angle_table(rows, cols):
    turns = np.mod(np.outer(rows.astype(np.int64), cols.astype(np.int64)), S).astype(np.float64)
    angles = turns * (2.0 * np.pi / S)
    return np.cos(angles).astype(np.float32), np.sin(angles).astype(np.float32)


def band_table():
    extent = NBINS + 2 * HALF
    bin_ids = np.arange(FIRST_BIN - HALF, FIRST_BIN - HALF + extent)
    inner = 128
    outer = S // inner
    cq, sq = angle_table(bin_ids, np.arange(outer) * inner)
    cr, sr = angle_table(bin_ids, np.arange(inner))
    cq, sq, cr, sr = (jnp.asarray(a) for a in (cq, sq, cr, sr))
    cos = cq[:, :, None] * cr[:, None, :] - sq[:, :, None] * sr[:, None, :]
    sin = sq[:, :, None] * cr[:, None, :] + cq[:, :, None] * sr[:, None, :]
    table = jnp.concatenate([cos, -sin], axis=0).astype(jnp.bfloat16)
    return table.reshape(2 * extent, S)


def lag_weights():
    bin_ids = FIRST_BIN + np.arange(NBINS)
    inner = 64
    outer = 2 * MAXLAG // inner
    ca, sa = angle_table(bin_ids, (np.arange(outer) - MAXLAG // inner) * inner)
    cb, sb = angle_table(bin_ids, np.arange(inner))
    ca, sa, cb, sb = (jnp.asarray(a) for a in (ca, sa, cb, sb))
    cos = ca[:, :, None] * cb[:, None, :] - sa[:, :, None] * sb[:, None, :]
    sin = sa[:, :, None] * cb[:, None, :] + ca[:, :, None] * sb[:, None, :]
    table = jnp.concatenate([cos, -sin], axis=0).astype(jnp.bfloat16)
    return table.reshape(2 * NBINS, 2 * MAXLAG)


def normalize(spectrum):
    extent = NBINS + 2 * HALF
    real_part = spectrum[:, :extent]
    imag_part = spectrum[:, extent:]
    magnitude = jnp.sqrt(real_part * real_part + imag_part * imag_part)
    smooth = magnitude[:, 0:NBINS]
    for offset in range(1, 2 * HALF + 1):
        smooth = smooth + magnitude[:, offset : offset + NBINS]
    smooth = smooth / (2 * HALF + 1) + 1e-06
    centre_re = real_part[:, HALF : HALF + NBINS] / smooth
    centre_im = imag_part[:, HALF : HALF + NBINS] / smooth
    return jnp.stack([centre_re, centre_im], axis=1).astype(jnp.bfloat16)


def whiten(row_data):
    spectrum = jnp.einsum("nt,kt->nk", row_data, band_table(), preferred_element_type=jnp.float32)
    return normalize(spectrum)


def cross_lhs(sources, receivers):
    src = sources.astype(jnp.float32)[:, :, :, :, None]
    rec = receivers.astype(jnp.float32)[:, None, :, None]
    windows = (0, 2)
    real_sum = jnp.sum(src[..., 0, :] * rec[..., 0, :] + src[..., 1, :] * rec[..., 1, :], axis=windows)
    imag_sum = jnp.sum(src[..., 1, :] * rec[..., 0, :] - src[..., 0, :] * rec[..., 1, :], axis=windows)
    lhs = jnp.stack([real_sum, imag_sum], axis=3).astype(jnp.bfloat16)
    return lhs.reshape(-1, 2 * NBINS)


def transform(lhs, weights, lag_scale, count_rec):
    result = jnp.dot(lhs, weights, preferred_element_type=jnp.float32) * lag_scale
    return result.reshape(-1, count_rec, 2 * MAXLAG)


def ring_stack(value, axis_name):
    size = lax.axis_size(axis_name)
    parts = [value] + [
        lax.ppermute(value, axis_name, [(i, (i + shift) % size) for i in range(size)])
        for shift in range(1, size)
    ]
    return jnp.stack(parts, 0)


def behind(axis_name, place):
    return (lax.axis_index(axis_name) - place) % lax.axis_size(axis_name)


def collect(own):
    part = ring_stack(own, "zh")
    for name in reversed(CHAN_AXES):
        part = ring_stack(part, name)
    part = ring_stack(part, "core")
    sizes = [lax.axis_size(name) for name in CHAN_AXES]
    flat = part.reshape((part.shape[0], -1) + part.shape[4:])
    place = jnp.arange(flat.shape[1], dtype=jnp.int32)
    arrived = 0
    for name, size in zip(CHAN_AXES, sizes):
        stride = flat.shape[1] // math.prod(sizes[: CHAN_AXES.index(name) + 1])
        arrived = arrived + behind(name, place // stride % size) * stride
    return jnp.take(flat, arrived, axis=1)


def per_device(records, source_rows):
    windows_here, rows_here, samples = records.shape
    whitened = whiten(records.reshape(windows_here * rows_here, samples)).reshape(
        windows_here, rows_here, 2, NBINS
    )
    shards = lax.axis_size(CHAN_AXES)
    block_len = source_rows.shape[1]
    per_shard = block_len // shards
    weights = lag_weights()
    lag_scale = math.sqrt(2.0 / (lax.axis_size(WIN_AXES) * windows_here * NBINS))
    receivers = lax.all_to_all(whitened, WIN_AXES, split_axis=1, concat_axis=0, tiled=True)
    shard = lax.axis_index(CHAN_AXES)
    own_rows = lax.dynamic_slice_in_dim(source_rows[0], shard * per_shard, per_shard)
    own_sources = jnp.take(whitened[0], own_rows, axis=0)
    sources = collect(own_sources)
    cores = lax.axis_size("core")
    core_s = jnp.arange(cores, dtype=jnp.int32)[:, None]
    zh_s = jnp.arange(lax.axis_size("zh"), dtype=jnp.int32)[None, :]
    window = behind("zh", zh_s) * cores + behind("core", core_s)
    receivers = jnp.take(receivers, window, axis=0)
    lhs = cross_lhs(sources, receivers)
    return transform(lhs, weights, lag_scale, receivers.shape[2])


def split_mesh(mesh):
    chan, win = mesh.shape["chan"], mesh.shape["win"]
    side = round(chan ** (1 / 3))
    devices = np.asarray(mesh.devices).reshape(side, side, chan // (side * side), win // 2, 2)
    return Mesh(devices, CHAN_AXES + WIN_AXES)


def solution(mesh):
    fine = split_mesh(mesh)
    in_specs = (P(WIN_AXES, CHAN_AXES, None), P())
    out_specs = P(None, CHAN_AXES + WIN_AXES, None)
    return jax.shard_map(
        per_device, mesh=fine, in_specs=in_specs, out_specs=out_specs, check_vma=False
    )
```

```python
import math

import numpy as np

import jax
import jax.numpy as jnp
from jax import lax
from jax.experimental import pallas as pl
from jax.sharding import Mesh, PartitionSpec as P

S = 7680
NBINS = 512
HALF = 32
FIRST_BIN = 64
MAXLAG = 1024

CHAN_AXES = ("y", "zl", "x")
WIN_AXES = ("zh", "core")


def angle_table(rows, cols):
    turns = np.mod(np.outer(rows.astype(np.int64), cols.astype(np.int64)), S).astype(np.float64)
    angles = turns * (2.0 * np.pi / S)
    return np.cos(angles).astype(np.float32), np.sin(angles).astype(np.float32)


TILE = 128
BIN_BLOCK = 128


def band_factors():
    extent = NBINS + 2 * HALF
    bin_ids = np.arange(FIRST_BIN - HALF, FIRST_BIN - HALF + extent)
    cq, sq = angle_table(bin_ids, np.arange(S // TILE) * TILE)
    cr, sr = angle_table(bin_ids, np.arange(TILE))
    a = np.concatenate([cq, -sq], axis=0)
    b = np.concatenate([-sq, -cq], axis=0)
    c = np.concatenate([cr, cr], axis=0)
    d = np.concatenate([sr, sr], axis=0)
    return tuple(jnp.asarray(v) for v in (a, b, c, d))


def dft_kernel(x_ref, a_ref, b_ref, c_ref, d_ref, o_ref):
    c = c_ref[...]
    d = d_ref[...]
    acc = jnp.zeros(o_ref.shape, jnp.float32)
    for q in range(S // TILE):
        twiddle = (a_ref[:, q : q + 1] * c + b_ref[:, q : q + 1] * d).astype(jnp.bfloat16)
        acc = acc + lax.dot_general(
            twiddle,
            x_ref[:, q * TILE : (q + 1) * TILE],
            (((1,), (1,)), ((), ())),
            preferred_element_type=jnp.float32,
        )
    o_ref[...] = acc


def band_spectrum(row_data):
    a, b, c, d = band_factors()
    bins = a.shape[0]
    rows = row_data.shape[0]
    out = pl.pallas_call(
        dft_kernel,
        out_shape=jax.ShapeDtypeStruct((bins, rows), jnp.float32),
        grid=(bins // BIN_BLOCK,),
        in_specs=[
            pl.BlockSpec((rows, S), lambda i: (0, 0)),
            pl.BlockSpec((BIN_BLOCK, a.shape[1]), lambda i: (i, 0)),
            pl.BlockSpec((BIN_BLOCK, b.shape[1]), lambda i: (i, 0)),
            pl.BlockSpec((BIN_BLOCK, TILE), lambda i: (i, 0)),
            pl.BlockSpec((BIN_BLOCK, TILE), lambda i: (i, 0)),
        ],
        out_specs=pl.BlockSpec((BIN_BLOCK, rows), lambda i: (i, 0)),
    )(row_data, a, b, c, d)
    return out.T


def lag_weights():
    bin_ids = FIRST_BIN + np.arange(NBINS)
    inner = 64
    outer = 2 * MAXLAG // inner
    ca, sa = angle_table(bin_ids, (np.arange(outer) - MAXLAG // inner) * inner)
    cb, sb = angle_table(bin_ids, np.arange(inner))
    ca, sa, cb, sb = (jnp.asarray(a) for a in (ca, sa, cb, sb))
    cos = ca[:, :, None] * cb[:, None, :] - sa[:, :, None] * sb[:, None, :]
    sin = sa[:, :, None] * cb[:, None, :] + ca[:, :, None] * sb[:, None, :]
    table = jnp.concatenate([cos, -sin], axis=0).astype(jnp.bfloat16)
    return table.reshape(2 * NBINS, 2 * MAXLAG)


def normalize(spectrum):
    extent = NBINS + 2 * HALF
    real_part = spectrum[:, :extent]
    imag_part = spectrum[:, extent:]
    magnitude = jnp.sqrt(real_part * real_part + imag_part * imag_part)
    smooth = magnitude[:, 0:NBINS]
    for offset in range(1, 2 * HALF + 1):
        smooth = smooth + magnitude[:, offset : offset + NBINS]
    smooth = smooth / (2 * HALF + 1) + 1e-06
    centre_re = real_part[:, HALF : HALF + NBINS] / smooth
    centre_im = imag_part[:, HALF : HALF + NBINS] / smooth
    return jnp.stack([centre_re, centre_im], axis=1).astype(jnp.bfloat16)


def whiten(row_data):
    return normalize(band_spectrum(row_data))


def cross_terms(source_part, receiver_part):
    real_sum = jnp.einsum(
        "wbi,wri->bri",
        source_part[:, :, 0],
        receiver_part[:, :, 0],
        preferred_element_type=jnp.float32,
    ) + jnp.einsum(
        "wbi,wri->bri",
        source_part[:, :, 1],
        receiver_part[:, :, 1],
        preferred_element_type=jnp.float32,
    )
    imag_sum = jnp.einsum(
        "wbi,wri->bri",
        source_part[:, :, 1],
        receiver_part[:, :, 0],
        preferred_element_type=jnp.float32,
    ) - jnp.einsum(
        "wbi,wri->bri",
        source_part[:, :, 0],
        receiver_part[:, :, 1],
        preferred_element_type=jnp.float32,
    )
    return jnp.stack([real_sum, imag_sum], axis=2)


def transform(spectra, weights, lag_scale):
    count_src, count_rec = (spectra.shape[0], spectra.shape[1])
    rounded = spectra.astype(jnp.bfloat16).reshape(count_src * count_rec, 2 * NBINS)
    result = jnp.dot(rounded, weights, preferred_element_type=jnp.float32) * lag_scale
    return result.reshape(count_src, count_rec, 2 * MAXLAG)


def ring_gather(value, axis_name, axis):
    size = lax.axis_size(axis_name)
    here = lax.axis_index(axis_name)
    parts = [value] + [
        lax.ppermute(value, axis_name, [(i, (i + shift) % size) for i in range(size)])
        for shift in range(1, size)
    ]
    stacked = jnp.stack(parts, 0)
    stacked = jnp.take(stacked, (here - jnp.arange(size)) % size, axis=0)
    stacked = jnp.moveaxis(stacked, 0, axis)
    shape = list(value.shape)
    shape[axis] *= size
    return stacked.reshape(shape)


def collect(own):
    part = ring_gather(own[None], "zh", 0)
    for name in reversed(CHAN_AXES):
        part = ring_gather(part, name, 2)
    part = ring_gather(part[None], "core", 0)
    part = jnp.swapaxes(part, 0, 1)
    return part.reshape(-1, part.shape[3], 2, NBINS)


def per_device(records, source_rows):
    windows_here, rows_here, samples = records.shape
    whitened = whiten(records.reshape(windows_here * rows_here, samples)).reshape(
        windows_here, rows_here, 2, NBINS
    )
    shards = lax.axis_size(CHAN_AXES)
    block_len = source_rows.shape[1]
    per_shard = block_len // shards
    weights = lag_weights()
    lag_scale = math.sqrt(2.0 / (lax.axis_size(WIN_AXES) * windows_here * NBINS))
    receivers = lax.all_to_all(whitened, WIN_AXES, split_axis=1, concat_axis=0, tiled=True)
    shard = lax.axis_index(CHAN_AXES)
    own_rows = lax.dynamic_slice_in_dim(source_rows[0], shard * per_shard, per_shard)
    own_sources = jnp.take(whitened, own_rows, axis=1)
    source_block = collect(own_sources)
    spectra = cross_terms(source_block, receivers)
    results = transform(spectra, weights, lag_scale)
    return results


def split_mesh(mesh):
    chan, win = mesh.shape["chan"], mesh.shape["win"]
    side = round(chan ** (1 / 3))
    devices = np.asarray(mesh.devices).reshape(side, side, chan // (side * side), win // 2, 2)
    return Mesh(devices, CHAN_AXES + WIN_AXES)


def solution(mesh):
    fine = split_mesh(mesh)
    in_specs = (P(WIN_AXES, CHAN_AXES, None), P())
    out_specs = P(None, CHAN_AXES + WIN_AXES, None)
    return jax.shard_map(
        per_device, mesh=fine, in_specs=in_specs, out_specs=out_specs, check_vma=False
    )
```

```python
import math

import ml_dtypes
import numpy as np

import jax
import jax.numpy as jnp
from jax import lax
from jax.sharding import Mesh, PartitionSpec as P

S = 7680
NBINS = 512
HALF = 32
FIRST_BIN = 64
MAXLAG = 1024

CHAN_AXES = ("y", "zl", "x")
WIN_AXES = ("zh", "core")


def angle_table(rows, cols):
    turns = np.mod(np.outer(rows.astype(np.int64), cols.astype(np.int64)), S).astype(np.float64)
    angles = turns * (2.0 * np.pi / S)
    return np.cos(angles).astype(np.float32), np.sin(angles).astype(np.float32)


def band_table():
    extent = NBINS + 2 * HALF
    bin_ids = np.arange(FIRST_BIN - HALF, FIRST_BIN - HALF + extent)
    cos, sin = angle_table(np.arange(S), bin_ids)
    table = np.concatenate([cos, -sin], axis=1).astype(ml_dtypes.bfloat16)
    return jnp.asarray(table)


def lag_weights():
    bin_ids = FIRST_BIN + np.arange(NBINS)
    inner = 64
    outer = 2 * MAXLAG // inner
    ca, sa = angle_table(bin_ids, (np.arange(outer) - MAXLAG // inner) * inner)
    cb, sb = angle_table(bin_ids, np.arange(inner))
    ca, sa, cb, sb = (jnp.asarray(a) for a in (ca, sa, cb, sb))
    cos = ca[:, :, None] * cb[:, None, :] - sa[:, :, None] * sb[:, None, :]
    sin = sa[:, :, None] * cb[:, None, :] + ca[:, :, None] * sb[:, None, :]
    table = jnp.concatenate([cos, -sin], axis=0).astype(jnp.bfloat16)
    return table.reshape(2 * NBINS, 2 * MAXLAG)


def normalize(spectrum):
    extent = NBINS + 2 * HALF
    real_part = spectrum[:, :extent]
    imag_part = spectrum[:, extent:]
    magnitude = jnp.sqrt(real_part * real_part + imag_part * imag_part)
    smooth = magnitude[:, 0:NBINS]
    for offset in range(1, 2 * HALF + 1):
        smooth = smooth + magnitude[:, offset : offset + NBINS]
    smooth = smooth / (2 * HALF + 1) + 1e-06
    centre_re = real_part[:, HALF : HALF + NBINS] / smooth
    centre_im = imag_part[:, HALF : HALF + NBINS] / smooth
    return jnp.stack([centre_re, centre_im], axis=1).astype(jnp.bfloat16)


def whiten(row_data):
    return normalize(jnp.dot(row_data, band_table(), preferred_element_type=jnp.float32))


def cross_terms(source_part, receiver_part):
    real_sum = jnp.einsum(
        "wbi,wri->bri",
        source_part[:, :, 0],
        receiver_part[:, :, 0],
        preferred_element_type=jnp.float32,
    ) + jnp.einsum(
        "wbi,wri->bri",
        source_part[:, :, 1],
        receiver_part[:, :, 1],
        preferred_element_type=jnp.float32,
    )
    imag_sum = jnp.einsum(
        "wbi,wri->bri",
        source_part[:, :, 1],
        receiver_part[:, :, 0],
        preferred_element_type=jnp.float32,
    ) - jnp.einsum(
        "wbi,wri->bri",
        source_part[:, :, 0],
        receiver_part[:, :, 1],
        preferred_element_type=jnp.float32,
    )
    return jnp.stack([real_sum, imag_sum], axis=2)


def transform(spectra, weights, lag_scale):
    count_src, count_rec = (spectra.shape[0], spectra.shape[1])
    rounded = spectra.astype(jnp.bfloat16).reshape(count_src * count_rec, 2 * NBINS)
    result = jnp.dot(rounded, weights, preferred_element_type=jnp.float32) * lag_scale
    return result.reshape(count_src, count_rec, 2 * MAXLAG)


def ring_gather(value, axis_name, axis):
    size = lax.axis_size(axis_name)
    here = lax.axis_index(axis_name)
    parts = [value] + [
        lax.ppermute(value, axis_name, [(i, (i + shift) % size) for i in range(size)])
        for shift in range(1, size)
    ]
    stacked = jnp.stack(parts, 0)
    stacked = jnp.take(stacked, (here - jnp.arange(size)) % size, axis=0)
    stacked = jnp.moveaxis(stacked, 0, axis)
    shape = list(value.shape)
    shape[axis] *= size
    return stacked.reshape(shape)


def collect(own):
    part = ring_gather(own[None], "zh", 0)
    for name in reversed(CHAN_AXES):
        part = ring_gather(part, name, 2)
    part = ring_gather(part[None], "core", 0)
    part = jnp.swapaxes(part, 0, 1)
    return part.reshape(-1, part.shape[3], 2, NBINS)


def per_device(records, source_rows):
    windows_here, rows_here, samples = records.shape
    whitened = whiten(records.reshape(windows_here * rows_here, samples)).reshape(
        windows_here, rows_here, 2, NBINS
    )
    shards = lax.axis_size(CHAN_AXES)
    block_len = source_rows.shape[1]
    per_shard = block_len // shards
    weights = lag_weights()
    lag_scale = math.sqrt(2.0 / (lax.axis_size(WIN_AXES) * windows_here * NBINS))
    receivers = lax.all_to_all(whitened, WIN_AXES, split_axis=1, concat_axis=0, tiled=True)
    shard = lax.axis_index(CHAN_AXES)
    own_rows = lax.dynamic_slice_in_dim(source_rows[0], shard * per_shard, per_shard)
    own_sources = jnp.take(whitened, own_rows, axis=1)
    source_block = collect(own_sources)
    spectra = cross_terms(source_block, receivers)
    results = transform(spectra, weights, lag_scale)
    return results


def split_mesh(mesh):
    chan, win = mesh.shape["chan"], mesh.shape["win"]
    side = round(chan ** (1 / 3))
    devices = np.asarray(mesh.devices).reshape(side, side, chan // (side * side), win // 2, 2)
    return Mesh(devices, CHAN_AXES + WIN_AXES)


def solution(mesh):
    fine = split_mesh(mesh)
    in_specs = (P(WIN_AXES, CHAN_AXES, None), P())
    out_specs = P(None, CHAN_AXES + WIN_AXES, None)
    return jax.shard_map(
        per_device, mesh=fine, in_specs=in_specs, out_specs=out_specs, check_vma=False
    )
```

```python
import math

import ml_dtypes
import numpy as np

import jax
import jax.numpy as jnp
from jax import lax
from jax.sharding import Mesh, PartitionSpec as P

S = 7680
NBINS = 512
HALF = 32
FIRST_BIN = 64
MAXLAG = 1024

CHAN_AXES = ("y", "zl", "x")
WIN_AXES = ("zh", "core")


def angle_table(rows, cols):
    turns = np.mod(np.outer(rows.astype(np.int64), cols.astype(np.int64)), S).astype(np.float64)
    angles = turns * (2.0 * np.pi / S)
    return np.cos(angles).astype(np.float32), np.sin(angles).astype(np.float32)


def band_table():
    extent = NBINS + 2 * HALF
    bin_ids = np.arange(FIRST_BIN - HALF, FIRST_BIN - HALF + extent)
    cos, sin = angle_table(np.arange(S), bin_ids)
    table = np.concatenate([cos, -sin], axis=1).astype(ml_dtypes.bfloat16)
    return jnp.asarray(table)


def lag_weights():
    bin_ids = FIRST_BIN + np.arange(NBINS)
    inner = 64
    outer = 2 * MAXLAG // inner
    ca, sa = angle_table(bin_ids, (np.arange(outer) - MAXLAG // inner) * inner)
    cb, sb = angle_table(bin_ids, np.arange(inner))
    ca, sa, cb, sb = (jnp.asarray(a) for a in (ca, sa, cb, sb))
    cos = ca[:, :, None] * cb[:, None, :] - sa[:, :, None] * sb[:, None, :]
    sin = sa[:, :, None] * cb[:, None, :] + ca[:, :, None] * sb[:, None, :]
    table = jnp.concatenate([cos, -sin], axis=0).astype(jnp.bfloat16)
    return table.reshape(2 * NBINS, 2 * MAXLAG)


def normalize(spectrum):
    extent = NBINS + 2 * HALF
    real_part = spectrum[:, :extent]
    imag_part = spectrum[:, extent:]
    magnitude = jnp.sqrt(real_part * real_part + imag_part * imag_part)
    smooth = magnitude[:, 0:NBINS]
    for offset in range(1, 2 * HALF + 1):
        smooth = smooth + magnitude[:, offset : offset + NBINS]
    smooth = smooth / (2 * HALF + 1) + 1e-06
    centre_re = real_part[:, HALF : HALF + NBINS] / smooth
    centre_im = imag_part[:, HALF : HALF + NBINS] / smooth
    return jnp.stack([centre_re, centre_im], axis=1).astype(jnp.bfloat16)


def whiten(row_data):
    return normalize(jnp.dot(row_data, band_table(), preferred_element_type=jnp.float32))


def cross_lhs(sources, receivers):
    src = sources.astype(jnp.float32)[:, :, None]
    rec = receivers.astype(jnp.float32)[:, None]
    real_sum = jnp.sum(src[..., 0, :] * rec[..., 0, :] + src[..., 1, :] * rec[..., 1, :], axis=0)
    imag_sum = jnp.sum(src[..., 1, :] * rec[..., 0, :] - src[..., 0, :] * rec[..., 1, :], axis=0)
    lhs = jnp.concatenate([real_sum, imag_sum], axis=2).reshape(-1, 2 * NBINS)
    return lhs.astype(jnp.bfloat16)


def transform(lhs, weights, lag_scale, count_rec):
    result = jnp.dot(lhs, weights, preferred_element_type=jnp.float32) * lag_scale
    return result.reshape(-1, count_rec, 2 * MAXLAG)


def ring_gather(value, axis_name, axis):
    size = lax.axis_size(axis_name)
    here = lax.axis_index(axis_name)
    shape = list(value.shape)
    block = shape[axis]
    shape[axis] *= size
    out = jnp.zeros(shape, value.dtype)
    for shift in range(size):
        part = value if shift == 0 else lax.ppermute(
            value, axis_name, [(i, (i + shift) % size) for i in range(size)]
        )
        start = [0] * len(shape)
        start[axis] = ((here - shift) % size) * block
        out = lax.dynamic_update_slice(out, part, start)
    return out


def collect(own):
    part = ring_gather(own, "zh", 0)
    for name in reversed(CHAN_AXES):
        part = ring_gather(part, name, 1)
    return ring_gather(part, "core", 0)


def per_device(records, source_rows):
    windows_here, rows_here, samples = records.shape
    whitened = whiten(records.reshape(windows_here * rows_here, samples)).reshape(
        windows_here, rows_here, 2, NBINS
    )
    shards = lax.axis_size(CHAN_AXES)
    block_len = source_rows.shape[1]
    per_shard = block_len // shards
    weights = lag_weights()
    lag_scale = math.sqrt(2.0 / (lax.axis_size(WIN_AXES) * windows_here * NBINS))
    receivers = lax.all_to_all(whitened, WIN_AXES, split_axis=1, concat_axis=0, tiled=True)
    receivers = jnp.swapaxes(
        receivers.reshape((lax.axis_size("zh"), lax.axis_size("core")) + receivers.shape[1:]), 0, 1
    ).reshape(receivers.shape)
    shard = lax.axis_index(CHAN_AXES)
    own_rows = lax.dynamic_slice_in_dim(source_rows[0], shard * per_shard, per_shard)
    own_sources = jnp.take(whitened, own_rows, axis=1)
    sources = collect(own_sources)
    lhs = cross_lhs(sources, receivers)
    return transform(lhs, weights, lag_scale, receivers.shape[1])


def split_mesh(mesh):
    chan, win = mesh.shape["chan"], mesh.shape["win"]
    side = round(chan ** (1 / 3))
    devices = np.asarray(mesh.devices).reshape(side, side, chan // (side * side), win // 2, 2)
    return Mesh(devices, CHAN_AXES + WIN_AXES)


def solution(mesh):
    fine = split_mesh(mesh)
    in_specs = (P(WIN_AXES, CHAN_AXES, None), P())
    out_specs = P(None, CHAN_AXES + WIN_AXES, None)
    return jax.shard_map(
        per_device, mesh=fine, in_specs=in_specs, out_specs=out_specs, check_vma=False
    )
```

```python
import math

import ml_dtypes
import numpy as np

import jax
import jax.numpy as jnp
from jax import lax
from jax.sharding import Mesh, PartitionSpec as P

S = 7680
NBINS = 512
HALF = 32
FIRST_BIN = 64
MAXLAG = 1024

CHAN_AXES = ("y", "zl", "x")
WIN_AXES = ("zh", "core")


def angle_table(rows, cols):
    turns = np.mod(np.outer(rows.astype(np.int64), cols.astype(np.int64)), S).astype(np.float64)
    angles = turns * (2.0 * np.pi / S)
    return np.cos(angles).astype(np.float32), np.sin(angles).astype(np.float32)


def band_table():
    extent = NBINS + 2 * HALF
    bin_ids = np.arange(FIRST_BIN - HALF, FIRST_BIN - HALF + extent)
    cos, sin = angle_table(np.arange(S), bin_ids)
    table = np.concatenate([cos, -sin], axis=1).astype(ml_dtypes.bfloat16)
    return jnp.asarray(table)


def lag_weights():
    bin_ids = FIRST_BIN + np.arange(NBINS)
    cos, sin = angle_table(bin_ids, np.arange(2 * MAXLAG) - MAXLAG)
    table = np.concatenate([cos, -sin], axis=0).astype(ml_dtypes.bfloat16)
    return jnp.asarray(table)


def normalize(spectrum):
    extent = NBINS + 2 * HALF
    real_part = spectrum[:, :extent]
    imag_part = spectrum[:, extent:]
    magnitude = jnp.sqrt(real_part * real_part + imag_part * imag_part)
    smooth = magnitude[:, 0:NBINS]
    for offset in range(1, 2 * HALF + 1):
        smooth = smooth + magnitude[:, offset : offset + NBINS]
    smooth = smooth / (2 * HALF + 1) + 1e-06
    centre_re = real_part[:, HALF : HALF + NBINS] / smooth
    centre_im = imag_part[:, HALF : HALF + NBINS] / smooth
    return jnp.stack([centre_re, centre_im], axis=1).astype(jnp.bfloat16)


def whiten(row_data):
    return normalize(jnp.dot(row_data, band_table(), preferred_element_type=jnp.float32))


def cross_lhs(sources, receivers):
    src = sources.astype(jnp.float32)[:, :, None]
    rec = receivers.astype(jnp.float32)[:, None]
    real_sum = jnp.sum(src[..., 0, :] * rec[..., 0, :] + src[..., 1, :] * rec[..., 1, :], axis=0)
    imag_sum = jnp.sum(src[..., 1, :] * rec[..., 0, :] - src[..., 0, :] * rec[..., 1, :], axis=0)
    lhs = jnp.concatenate([real_sum, imag_sum], axis=2).reshape(-1, 2 * NBINS)
    return lhs.astype(jnp.bfloat16)


def transform(lhs, weights, lag_scale, count_rec):
    result = jnp.dot(lhs, weights, preferred_element_type=jnp.float32) * lag_scale
    return result.reshape(-1, count_rec, 2 * MAXLAG)


def ring_gather(value, axis_name, axis):
    size = lax.axis_size(axis_name)
    here = lax.axis_index(axis_name)
    shape = list(value.shape)
    block = shape[axis]
    shape[axis] *= size
    out = jnp.zeros(shape, value.dtype)
    for shift in range(size):
        part = value if shift == 0 else lax.ppermute(
            value, axis_name, [(i, (i + shift) % size) for i in range(size)]
        )
        start = [0] * len(shape)
        start[axis] = ((here - shift) % size) * block
        out = lax.dynamic_update_slice(out, part, start)
    return out


def collect(own):
    part = ring_gather(own, "zh", 0)
    for name in reversed(CHAN_AXES):
        part = ring_gather(part, name, 1)
    return ring_gather(part, "core", 0)


def per_device(records, source_rows):
    windows_here, rows_here, samples = records.shape
    whitened = whiten(records.reshape(windows_here * rows_here, samples)).reshape(
        windows_here, rows_here, 2, NBINS
    )
    shards = lax.axis_size(CHAN_AXES)
    block_len = source_rows.shape[1]
    per_shard = block_len // shards
    weights = lag_weights()
    lag_scale = math.sqrt(2.0 / (lax.axis_size(WIN_AXES) * windows_here * NBINS))
    receivers = lax.all_to_all(whitened, WIN_AXES, split_axis=1, concat_axis=0, tiled=True)
    receivers = jnp.swapaxes(
        receivers.reshape((lax.axis_size("zh"), lax.axis_size("core")) + receivers.shape[1:]), 0, 1
    ).reshape(receivers.shape)
    shard = lax.axis_index(CHAN_AXES)
    own_rows = lax.dynamic_slice_in_dim(source_rows[0], shard * per_shard, per_shard)
    own_sources = jnp.take(whitened, own_rows, axis=1)
    sources = collect(own_sources)
    lhs = cross_lhs(sources, receivers)
    return transform(lhs, weights, lag_scale, receivers.shape[1])


def split_mesh(mesh):
    chan, win = mesh.shape["chan"], mesh.shape["win"]
    side = round(chan ** (1 / 3))
    devices = np.asarray(mesh.devices).reshape(side, side, chan // (side * side), win // 2, 2)
    return Mesh(devices, CHAN_AXES + WIN_AXES)


def solution(mesh):
    fine = split_mesh(mesh)
    in_specs = (P(WIN_AXES, CHAN_AXES, None), P())
    out_specs = P(None, CHAN_AXES + WIN_AXES, None)
    return jax.shard_map(
        per_device, mesh=fine, in_specs=in_specs, out_specs=out_specs, check_vma=False
    )
```

```python
import math

import ml_dtypes
import numpy as np

import jax
import jax.numpy as jnp
from jax import lax
from jax.sharding import Mesh, PartitionSpec as P

S = 7680
NBINS = 512
HALF = 32
FIRST_BIN = 64
MAXLAG = 1024

CHAN_AXES = ("y", "zl", "x")
WIN_AXES = ("zh", "core")


def angle_table(rows, cols):
    turns = np.mod(np.outer(rows.astype(np.int64), cols.astype(np.int64)), S).astype(np.float64)
    angles = turns * (2.0 * np.pi / S)
    return np.cos(angles).astype(np.float32), np.sin(angles).astype(np.float32)


def band_table():
    extent = NBINS + 2 * HALF
    bin_ids = np.arange(FIRST_BIN - HALF, FIRST_BIN - HALF + extent)
    cos, sin = angle_table(np.arange(S), bin_ids)
    table = np.concatenate([cos, -sin], axis=1).astype(ml_dtypes.bfloat16)
    return jnp.asarray(table)


def lag_weights():
    bin_ids = FIRST_BIN + np.arange(NBINS)
    inner = 64
    outer = 2 * MAXLAG // inner
    ca, sa = angle_table(bin_ids, (np.arange(outer) - MAXLAG // inner) * inner)
    cb, sb = angle_table(bin_ids, np.arange(inner))
    ca, sa, cb, sb = (jnp.asarray(a) for a in (ca, sa, cb, sb))
    cos = ca[:, :, None] * cb[:, None, :] - sa[:, :, None] * sb[:, None, :]
    sin = sa[:, :, None] * cb[:, None, :] + ca[:, :, None] * sb[:, None, :]
    table = jnp.concatenate([cos, -sin], axis=0).astype(jnp.bfloat16)
    return table.reshape(2 * NBINS, 2 * MAXLAG)


def normalize(spectrum):
    extent = NBINS + 2 * HALF
    real_part = spectrum[:, :extent]
    imag_part = spectrum[:, extent:]
    magnitude = jnp.sqrt(real_part * real_part + imag_part * imag_part)
    smooth = magnitude[:, 0:NBINS]
    for offset in range(1, 2 * HALF + 1):
        smooth = smooth + magnitude[:, offset : offset + NBINS]
    smooth = smooth / (2 * HALF + 1) + 1e-06
    centre_re = real_part[:, HALF : HALF + NBINS] / smooth
    centre_im = imag_part[:, HALF : HALF + NBINS] / smooth
    return jnp.stack([centre_re, centre_im], axis=1).astype(jnp.bfloat16)


def whiten(row_data):
    return normalize(jnp.dot(row_data, band_table(), preferred_element_type=jnp.float32))


def cross_lhs(sources, receivers):
    src = sources.astype(jnp.float32)[:, :, None]
    rec = receivers.astype(jnp.float32)[:, None]
    real_sum = jnp.sum(src[..., 0, :] * rec[..., 0, :] + src[..., 1, :] * rec[..., 1, :], axis=0)
    imag_sum = jnp.sum(src[..., 1, :] * rec[..., 0, :] - src[..., 0, :] * rec[..., 1, :], axis=0)
    lhs = jnp.concatenate([real_sum, imag_sum], axis=2).reshape(-1, 2 * NBINS)
    return lhs.astype(jnp.bfloat16)


def transform(lhs, weights, lag_scale, count_rec):
    result = jnp.dot(lhs, weights, preferred_element_type=jnp.float32) * lag_scale
    return result.reshape(-1, count_rec, 2 * MAXLAG)


def ring_gather(value, axis_name, axis):
    size = lax.axis_size(axis_name)
    here = lax.axis_index(axis_name)
    shape = list(value.shape)
    block = shape[axis]
    shape[axis] *= size
    out = jnp.zeros(shape, value.dtype)
    for shift in range(size):
        part = value if shift == 0 else lax.ppermute(
            value, axis_name, [(i, (i + shift) % size) for i in range(size)]
        )
        start = [0] * len(shape)
        start[axis] = ((here - shift) % size) * block
        out = lax.dynamic_update_slice(out, part, start)
    return out


def collect(own):
    part = ring_gather(own, "zh", 0)
    for name in reversed(CHAN_AXES):
        part = ring_gather(part, name, 1)
    return ring_gather(part, "core", 0)


def exchange_receivers(rows):
    here = lax.axis_index(WIN_AXES)
    count = lax.axis_size(WIN_AXES)
    cores = lax.axis_size("core")
    quarter = rows.shape[0] // count
    out = jnp.zeros((count, quarter) + rows.shape[1:], rows.dtype)
    for shift in range(count):
        block = lax.dynamic_slice_in_dim(rows, ((here + shift) % count) * quarter, quarter)
        if shift:
            block = lax.ppermute(block, WIN_AXES, [(i, (i + shift) % count) for i in range(count)])
        origin = (here - shift) % count
        place = (origin % cores) * (count // cores) + origin // cores
        out = lax.dynamic_update_slice(out, block[None], (place, 0, 0, 0))
    return out


def per_device(records, source_rows):
    windows_here, rows_here, samples = records.shape
    whitened = whiten(records.reshape(windows_here * rows_here, samples)).reshape(
        windows_here, rows_here, 2, NBINS
    )
    shards = lax.axis_size(CHAN_AXES)
    block_len = source_rows.shape[1]
    per_shard = block_len // shards
    weights = lag_weights()
    lag_scale = math.sqrt(2.0 / (lax.axis_size(WIN_AXES) * windows_here * NBINS))
    receivers = exchange_receivers(whitened[0])
    shard = lax.axis_index(CHAN_AXES)
    own_rows = lax.dynamic_slice_in_dim(source_rows[0], shard * per_shard, per_shard)
    own_sources = jnp.take(whitened, own_rows, axis=1)
    sources = collect(own_sources)
    lhs = cross_lhs(sources, receivers)
    return transform(lhs, weights, lag_scale, receivers.shape[1])


def split_mesh(mesh):
    chan, win = mesh.shape["chan"], mesh.shape["win"]
    side = round(chan ** (1 / 3))
    devices = np.asarray(mesh.devices).reshape(side, side, chan // (side * side), win // 2, 2)
    return Mesh(devices, CHAN_AXES + WIN_AXES)


def solution(mesh):
    fine = split_mesh(mesh)
    in_specs = (P(WIN_AXES, CHAN_AXES, None), P())
    out_specs = P(None, CHAN_AXES + WIN_AXES, None)
    return jax.shard_map(
        per_device, mesh=fine, in_specs=in_specs, out_specs=out_specs, check_vma=False
    )
```

```python
import functools
import math

import ml_dtypes
import numpy as np

import jax
import jax.numpy as jnp
from jax import lax
from jax.experimental import pallas as pl
from jax.sharding import Mesh, PartitionSpec as P

S = 7680
NBINS = 512
HALF = 32
FIRST_BIN = 64
MAXLAG = 1024

CHAN_AXES = ("y", "zl", "x")
WIN_AXES = ("zh", "core")


def angle_table(rows, cols):
    turns = np.mod(np.outer(rows.astype(np.int64), cols.astype(np.int64)), S).astype(np.float64)
    angles = turns * (2.0 * np.pi / S)
    return np.cos(angles).astype(np.float32), np.sin(angles).astype(np.float32)


def band_table():
    extent = NBINS + 2 * HALF
    bin_ids = np.arange(FIRST_BIN - HALF, FIRST_BIN - HALF + extent)
    cos, sin = angle_table(np.arange(S), bin_ids)
    table = np.concatenate([cos, -sin], axis=1).astype(ml_dtypes.bfloat16)
    return jnp.asarray(table)


def lag_weights():
    bin_ids = FIRST_BIN + np.arange(NBINS)
    inner = 64
    outer = 2 * MAXLAG // inner
    ca, sa = angle_table(bin_ids, (np.arange(outer) - MAXLAG // inner) * inner)
    cb, sb = angle_table(bin_ids, np.arange(inner))
    ca, sa, cb, sb = (jnp.asarray(a) for a in (ca, sa, cb, sb))
    cos = ca[:, :, None] * cb[:, None, :] - sa[:, :, None] * sb[:, None, :]
    sin = sa[:, :, None] * cb[:, None, :] + ca[:, :, None] * sb[:, None, :]
    table = jnp.concatenate([cos, -sin], axis=0).astype(jnp.bfloat16)
    return table.reshape(2 * NBINS, 2 * MAXLAG)


def normalize(spectrum):
    extent = NBINS + 2 * HALF
    real_part = spectrum[:, :extent]
    imag_part = spectrum[:, extent:]
    magnitude = jnp.sqrt(real_part * real_part + imag_part * imag_part)
    smooth = magnitude[:, 0:NBINS]
    for offset in range(1, 2 * HALF + 1):
        smooth = smooth + magnitude[:, offset : offset + NBINS]
    smooth = smooth / (2 * HALF + 1) + 1e-06
    centre_re = real_part[:, HALF : HALF + NBINS] / smooth
    centre_im = imag_part[:, HALF : HALF + NBINS] / smooth
    return jnp.stack([centre_re, centre_im], axis=1).astype(jnp.bfloat16)


def whiten(row_data):
    return normalize(jnp.dot(row_data, band_table(), preferred_element_type=jnp.float32))


def cross_lhs(sources, receivers):
    src = sources.astype(jnp.float32)[:, :, None]
    rec = receivers.astype(jnp.float32)[:, None]
    real_sum = jnp.sum(src[..., 0, :] * rec[..., 0, :] + src[..., 1, :] * rec[..., 1, :], axis=0)
    imag_sum = jnp.sum(src[..., 1, :] * rec[..., 0, :] - src[..., 0, :] * rec[..., 1, :], axis=0)
    lhs = jnp.concatenate([real_sum, imag_sum], axis=2).reshape(-1, 2 * NBINS)
    return lhs.astype(jnp.bfloat16)


SOURCE_BLOCK = 32


def lag_kernel(lhs_ref, w_ref, o_ref, *, scale):
    result = jnp.dot(lhs_ref[...], w_ref[...], preferred_element_type=jnp.float32) * scale
    o_ref[...] = result.reshape(o_ref.shape)


def transform(lhs, weights, lag_scale, count_rec):
    count_src = lhs.shape[0] // count_rec
    rows = SOURCE_BLOCK * count_rec
    return pl.pallas_call(
        functools.partial(lag_kernel, scale=lag_scale),
        out_shape=jax.ShapeDtypeStruct((count_src, count_rec, 2 * MAXLAG), jnp.float32),
        grid=(count_src // SOURCE_BLOCK,),
        in_specs=[
            pl.BlockSpec((rows, lhs.shape[1]), lambda i: (i, 0)),
            pl.BlockSpec(weights.shape, lambda i: (0, 0)),
        ],
        out_specs=pl.BlockSpec((SOURCE_BLOCK, count_rec, 2 * MAXLAG), lambda i: (i, 0, 0)),
    )(lhs, weights)


def ring_gather(value, axis_name, axis):
    size = lax.axis_size(axis_name)
    here = lax.axis_index(axis_name)
    shape = list(value.shape)
    block = shape[axis]
    shape[axis] *= size
    out = jnp.zeros(shape, value.dtype)
    for shift in range(size):
        part = value if shift == 0 else lax.ppermute(
            value, axis_name, [(i, (i + shift) % size) for i in range(size)]
        )
        start = [0] * len(shape)
        start[axis] = ((here - shift) % size) * block
        out = lax.dynamic_update_slice(out, part, start)
    return out


def collect(own):
    part = ring_gather(own, "zh", 0)
    for name in reversed(CHAN_AXES):
        part = ring_gather(part, name, 1)
    return ring_gather(part, "core", 0)


def exchange_receivers(rows):
    here = lax.axis_index(WIN_AXES)
    count = lax.axis_size(WIN_AXES)
    cores = lax.axis_size("core")
    quarter = rows.shape[0] // count
    out = jnp.zeros((count, quarter) + rows.shape[1:], rows.dtype)
    for shift in range(count):
        block = lax.dynamic_slice_in_dim(rows, ((here + shift) % count) * quarter, quarter)
        if shift:
            block = lax.ppermute(block, WIN_AXES, [(i, (i + shift) % count) for i in range(count)])
        origin = (here - shift) % count
        place = (origin % cores) * (count // cores) + origin // cores
        out = lax.dynamic_update_slice(out, block[None], (place, 0, 0, 0))
    return out


def per_device(records, source_rows):
    windows_here, rows_here, samples = records.shape
    whitened = whiten(records.reshape(windows_here * rows_here, samples)).reshape(
        windows_here, rows_here, 2, NBINS
    )
    shards = lax.axis_size(CHAN_AXES)
    block_len = source_rows.shape[1]
    per_shard = block_len // shards
    weights = lag_weights()
    lag_scale = math.sqrt(2.0 / (lax.axis_size(WIN_AXES) * windows_here * NBINS))
    receivers = exchange_receivers(whitened[0])
    shard = lax.axis_index(CHAN_AXES)
    own_rows = lax.dynamic_slice_in_dim(source_rows[0], shard * per_shard, per_shard)
    own_sources = jnp.take(whitened, own_rows, axis=1)
    sources = collect(own_sources)
    lhs = cross_lhs(sources, receivers)
    return transform(lhs, weights, lag_scale, receivers.shape[1])


def split_mesh(mesh):
    chan, win = mesh.shape["chan"], mesh.shape["win"]
    side = round(chan ** (1 / 3))
    devices = np.asarray(mesh.devices).reshape(side, side, chan // (side * side), win // 2, 2)
    return Mesh(devices, CHAN_AXES + WIN_AXES)


def solution(mesh):
    fine = split_mesh(mesh)
    in_specs = (P(WIN_AXES, CHAN_AXES, None), P())
    out_specs = P(None, CHAN_AXES + WIN_AXES, None)
    return jax.shard_map(
        per_device, mesh=fine, in_specs=in_specs, out_specs=out_specs, check_vma=False
    )
```

```python
import functools
import math

import ml_dtypes
import numpy as np

import jax
import jax.numpy as jnp
from jax import lax
from jax.experimental import pallas as pl
from jax.sharding import Mesh, PartitionSpec as P

S = 7680
NBINS = 512
HALF = 32
FIRST_BIN = 64
MAXLAG = 1024

CHAN_AXES = ("y", "zl", "x")
WIN_AXES = ("zh", "core")


def angle_table(rows, cols):
    turns = np.mod(np.outer(rows.astype(np.int64), cols.astype(np.int64)), S).astype(np.float64)
    angles = turns * (2.0 * np.pi / S)
    return np.cos(angles).astype(np.float32), np.sin(angles).astype(np.float32)


def band_table():
    extent = NBINS + 2 * HALF
    bin_ids = np.arange(FIRST_BIN - HALF, FIRST_BIN - HALF + extent)
    cos, sin = angle_table(np.arange(S), bin_ids)
    table = np.concatenate([cos, -sin], axis=1).astype(ml_dtypes.bfloat16)
    return jnp.asarray(table)


def lag_weights():
    bin_ids = FIRST_BIN + np.arange(NBINS)
    cos, sin = angle_table(bin_ids, np.arange(2 * MAXLAG) - MAXLAG)
    table = np.concatenate([cos, -sin], axis=0).astype(ml_dtypes.bfloat16)
    return jnp.asarray(table)


def normalize(spectrum):
    extent = NBINS + 2 * HALF
    real_part = spectrum[:, :extent]
    imag_part = spectrum[:, extent:]
    magnitude = jnp.sqrt(real_part * real_part + imag_part * imag_part)
    smooth = magnitude[:, 0:NBINS]
    for offset in range(1, 2 * HALF + 1):
        smooth = smooth + magnitude[:, offset : offset + NBINS]
    smooth = smooth / (2 * HALF + 1) + 1e-06
    centre_re = real_part[:, HALF : HALF + NBINS] / smooth
    centre_im = imag_part[:, HALF : HALF + NBINS] / smooth
    return jnp.stack([centre_re, centre_im], axis=1).astype(jnp.bfloat16)


def whiten(row_data):
    return normalize(jnp.dot(row_data, band_table(), preferred_element_type=jnp.float32))


def cross_lhs(sources, receivers):
    src = sources.astype(jnp.float32)[:, :, None]
    rec = receivers.astype(jnp.float32)[:, None]
    real_sum = jnp.sum(src[..., 0, :] * rec[..., 0, :] + src[..., 1, :] * rec[..., 1, :], axis=0)
    imag_sum = jnp.sum(src[..., 1, :] * rec[..., 0, :] - src[..., 0, :] * rec[..., 1, :], axis=0)
    lhs = jnp.concatenate([real_sum, imag_sum], axis=2).reshape(-1, 2 * NBINS)
    return lhs.astype(jnp.bfloat16)


SOURCE_BLOCK = 32


def lag_kernel(lhs_ref, w_ref, o_ref, *, scale):
    result = jnp.dot(lhs_ref[...], w_ref[...], preferred_element_type=jnp.float32) * scale
    o_ref[...] = result.reshape(o_ref.shape)


def transform(lhs, weights, lag_scale, count_rec):
    count_src = lhs.shape[0] // count_rec
    rows = SOURCE_BLOCK * count_rec
    return pl.pallas_call(
        functools.partial(lag_kernel, scale=lag_scale),
        out_shape=jax.ShapeDtypeStruct((count_src, count_rec, 2 * MAXLAG), jnp.float32),
        grid=(count_src // SOURCE_BLOCK,),
        in_specs=[
            pl.BlockSpec((rows, lhs.shape[1]), lambda i: (i, 0)),
            pl.BlockSpec(weights.shape, lambda i: (0, 0)),
        ],
        out_specs=pl.BlockSpec((SOURCE_BLOCK, count_rec, 2 * MAXLAG), lambda i: (i, 0, 0)),
    )(lhs, weights)


def ring_gather(value, axis_name, axis):
    size = lax.axis_size(axis_name)
    here = lax.axis_index(axis_name)
    shape = list(value.shape)
    block = shape[axis]
    shape[axis] *= size
    out = jnp.zeros(shape, value.dtype)
    for shift in range(size):
        part = value if shift == 0 else lax.ppermute(
            value, axis_name, [(i, (i + shift) % size) for i in range(size)]
        )
        start = [0] * len(shape)
        start[axis] = ((here - shift) % size) * block
        out = lax.dynamic_update_slice(out, part, start)
    return out


def collect(own):
    part = ring_gather(own, "zh", 0)
    for name in reversed(CHAN_AXES):
        part = ring_gather(part, name, 1)
    return ring_gather(part, "core", 0)


def exchange_receivers(rows):
    here = lax.axis_index(WIN_AXES)
    count = lax.axis_size(WIN_AXES)
    cores = lax.axis_size("core")
    quarter = rows.shape[0] // count
    out = jnp.zeros((count, quarter) + rows.shape[1:], rows.dtype)
    for shift in range(count):
        block = lax.dynamic_slice_in_dim(rows, ((here + shift) % count) * quarter, quarter)
        if shift:
            block = lax.ppermute(block, WIN_AXES, [(i, (i + shift) % count) for i in range(count)])
        origin = (here - shift) % count
        place = (origin % cores) * (count // cores) + origin // cores
        out = lax.dynamic_update_slice(out, block[None], (place, 0, 0, 0))
    return out


def per_device(records, source_rows):
    windows_here, rows_here, samples = records.shape
    whitened = whiten(records.reshape(windows_here * rows_here, samples)).reshape(
        windows_here, rows_here, 2, NBINS
    )
    shards = lax.axis_size(CHAN_AXES)
    block_len = source_rows.shape[1]
    per_shard = block_len // shards
    weights = lag_weights()
    lag_scale = math.sqrt(2.0 / (lax.axis_size(WIN_AXES) * windows_here * NBINS))
    receivers = exchange_receivers(whitened[0])
    shard = lax.axis_index(CHAN_AXES)
    own_rows = lax.dynamic_slice_in_dim(source_rows[0], shard * per_shard, per_shard)
    own_sources = jnp.take(whitened, own_rows, axis=1)
    sources = collect(own_sources)
    lhs = cross_lhs(sources, receivers)
    return transform(lhs, weights, lag_scale, receivers.shape[1])


def split_mesh(mesh):
    chan, win = mesh.shape["chan"], mesh.shape["win"]
    side = round(chan ** (1 / 3))
    devices = np.asarray(mesh.devices).reshape(side, side, chan // (side * side), win // 2, 2)
    return Mesh(devices, CHAN_AXES + WIN_AXES)


def solution(mesh):
    fine = split_mesh(mesh)
    in_specs = (P(WIN_AXES, CHAN_AXES, None), P())
    out_specs = P(None, CHAN_AXES + WIN_AXES, None)
    return jax.shard_map(
        per_device, mesh=fine, in_specs=in_specs, out_specs=out_specs, check_vma=False
    )
```

```python
import functools
import math

import ml_dtypes
import numpy as np

import jax
import jax.numpy as jnp
from jax import lax
from jax.experimental import pallas as pl
from jax.sharding import Mesh, PartitionSpec as P

S = 7680
NBINS = 512
HALF = 32
FIRST_BIN = 64
MAXLAG = 1024

CHAN_AXES = ("y", "zl", "x")
WIN_AXES = ("zh", "core")


def angle_table(rows, cols):
    turns = np.mod(np.outer(rows.astype(np.int64), cols.astype(np.int64)), S).astype(np.float64)
    angles = turns * (2.0 * np.pi / S)
    return np.cos(angles).astype(np.float32), np.sin(angles).astype(np.float32)


def band_table():
    extent = NBINS + 2 * HALF
    bin_ids = np.arange(FIRST_BIN - HALF, FIRST_BIN - HALF + extent)
    cos, sin = angle_table(np.arange(S), bin_ids)
    table = np.concatenate([cos, -sin], axis=1).astype(ml_dtypes.bfloat16)
    return jnp.asarray(table)


def lag_weights():
    bin_ids = FIRST_BIN + np.arange(NBINS)
    cos, sin = angle_table(bin_ids, np.arange(2 * MAXLAG) - MAXLAG)
    table = np.concatenate([cos, -sin], axis=0).astype(ml_dtypes.bfloat16)
    return jnp.asarray(table)


def normalize(spectrum):
    extent = NBINS + 2 * HALF
    real_part = spectrum[:, :extent]
    imag_part = spectrum[:, extent:]
    magnitude = jnp.sqrt(real_part * real_part + imag_part * imag_part)
    smooth = magnitude[:, 0:NBINS]
    for offset in range(1, 2 * HALF + 1):
        smooth = smooth + magnitude[:, offset : offset + NBINS]
    smooth = smooth / (2 * HALF + 1) + 1e-06
    centre_re = real_part[:, HALF : HALF + NBINS] / smooth
    centre_im = imag_part[:, HALF : HALF + NBINS] / smooth
    return jnp.stack([centre_re, centre_im], axis=1).astype(jnp.bfloat16)


def whiten(row_data):
    return normalize(jnp.dot(row_data, band_table(), preferred_element_type=jnp.float32))


def cross_lhs(sources, receivers):
    src = sources.astype(jnp.float32)[:, :, None]
    rec = receivers.astype(jnp.float32)[:, None]
    real_sum = jnp.sum(src[..., 0, :] * rec[..., 0, :] + src[..., 1, :] * rec[..., 1, :], axis=0)
    imag_sum = jnp.sum(src[..., 1, :] * rec[..., 0, :] - src[..., 0, :] * rec[..., 1, :], axis=0)
    lhs = jnp.concatenate([real_sum, imag_sum], axis=2).reshape(-1, 2 * NBINS)
    return lhs.astype(jnp.bfloat16)


SOURCE_BLOCK = 32


def lag_kernel(lhs_ref, w_ref, o_ref, *, scale):
    result = jnp.dot(lhs_ref[...], w_ref[...], preferred_element_type=jnp.float32) * scale
    o_ref[...] = result.reshape(o_ref.shape)


def transform(lhs, weights, lag_scale, count_rec):
    count_src = lhs.shape[0] // count_rec
    rows = SOURCE_BLOCK * count_rec
    return pl.pallas_call(
        functools.partial(lag_kernel, scale=lag_scale),
        out_shape=jax.ShapeDtypeStruct((count_src, count_rec, 2 * MAXLAG), jnp.float32),
        grid=(count_src // SOURCE_BLOCK,),
        in_specs=[
            pl.BlockSpec((rows, lhs.shape[1]), lambda i: (i, 0)),
            pl.BlockSpec(weights.shape, lambda i: (0, 0)),
        ],
        out_specs=pl.BlockSpec((SOURCE_BLOCK, count_rec, 2 * MAXLAG), lambda i: (i, 0, 0)),
    )(lhs, weights)


def group_gather(value, names, axes):
    sizes = [lax.axis_size(name) for name in names]
    total = math.prod(sizes)
    here = lax.axis_index(tuple(names))
    shape = list(value.shape)
    for name, axis in zip(names, axes):
        shape[axis] *= lax.axis_size(name)
    out = jnp.zeros(shape, value.dtype)
    for shift in range(total):
        part = value if shift == 0 else lax.ppermute(
            value, tuple(names), [(i, (i + shift) % total) for i in range(total)]
        )
        origin = (here - shift) % total
        start = [0] * len(shape)
        for k, (name, axis) in enumerate(zip(names, axes)):
            coord = origin // math.prod(sizes[k + 1 :]) % sizes[k]
            later = [s for s, a in zip(sizes[k + 1 :], axes[k + 1 :]) if a == axis]
            start[axis] = start[axis] + coord * math.prod(later) * value.shape[axis]
        out = lax.dynamic_update_slice(out, part, start)
    return out


def collect(own):
    part = group_gather(own, ("x", "zh"), (1, 0))
    part = group_gather(part, ("y", "zl"), (1, 1))
    return group_gather(part, ("core",), (0,))


def exchange_receivers(rows):
    here = lax.axis_index(WIN_AXES)
    count = lax.axis_size(WIN_AXES)
    cores = lax.axis_size("core")
    quarter = rows.shape[0] // count
    out = jnp.zeros((count, quarter) + rows.shape[1:], rows.dtype)
    for shift in range(count):
        block = lax.dynamic_slice_in_dim(rows, ((here + shift) % count) * quarter, quarter)
        if shift:
            block = lax.ppermute(block, WIN_AXES, [(i, (i + shift) % count) for i in range(count)])
        origin = (here - shift) % count
        place = (origin % cores) * (count // cores) + origin // cores
        out = lax.dynamic_update_slice(out, block[None], (place, 0, 0, 0))
    return out


def per_device(records, source_rows):
    windows_here, rows_here, samples = records.shape
    whitened = whiten(records.reshape(windows_here * rows_here, samples)).reshape(
        windows_here, rows_here, 2, NBINS
    )
    shards = lax.axis_size(CHAN_AXES)
    block_len = source_rows.shape[1]
    per_shard = block_len // shards
    weights = lag_weights()
    lag_scale = math.sqrt(2.0 / (lax.axis_size(WIN_AXES) * windows_here * NBINS))
    receivers = exchange_receivers(whitened[0])
    shard = lax.axis_index(CHAN_AXES)
    own_rows = lax.dynamic_slice_in_dim(source_rows[0], shard * per_shard, per_shard)
    own_sources = jnp.take(whitened, own_rows, axis=1)
    sources = collect(own_sources)
    lhs = cross_lhs(sources, receivers)
    return transform(lhs, weights, lag_scale, receivers.shape[1])


def split_mesh(mesh):
    chan, win = mesh.shape["chan"], mesh.shape["win"]
    side = round(chan ** (1 / 3))
    devices = np.asarray(mesh.devices).reshape(side, side, chan // (side * side), win // 2, 2)
    return Mesh(devices, CHAN_AXES + WIN_AXES)


def solution(mesh):
    fine = split_mesh(mesh)
    in_specs = (P(WIN_AXES, CHAN_AXES, None), P())
    out_specs = P(None, CHAN_AXES + WIN_AXES, None)
    return jax.shard_map(
        per_device, mesh=fine, in_specs=in_specs, out_specs=out_specs, check_vma=False
    )
```

```python
import functools
import math

import ml_dtypes
import numpy as np

import jax
import jax.numpy as jnp
from jax import lax
from jax.experimental import pallas as pl
from jax.sharding import Mesh, PartitionSpec as P

S = 7680
NBINS = 512
HALF = 32
FIRST_BIN = 64
MAXLAG = 1024

CHAN_AXES = ("y", "zl", "x")
WIN_AXES = ("zh", "core")


def angle_table(rows, cols):
    turns = np.mod(np.outer(rows.astype(np.int64), cols.astype(np.int64)), S).astype(np.float64)
    angles = turns * (2.0 * np.pi / S)
    return np.cos(angles).astype(np.float32), np.sin(angles).astype(np.float32)


def band_table():
    extent = NBINS + 2 * HALF
    bin_ids = np.arange(FIRST_BIN - HALF, FIRST_BIN - HALF + extent)
    cos, sin = angle_table(np.arange(S), bin_ids)
    table = np.concatenate([cos, -sin], axis=1).astype(ml_dtypes.bfloat16)
    return jnp.asarray(table)


def lag_weights():
    bin_ids = FIRST_BIN + np.arange(NBINS)
    cos, sin = angle_table(bin_ids, np.arange(2 * MAXLAG) - MAXLAG)
    table = np.concatenate([cos, -sin], axis=0).astype(ml_dtypes.bfloat16)
    return jnp.asarray(table)


def normalize(spectrum):
    extent = NBINS + 2 * HALF
    real_part = spectrum[:, :extent]
    imag_part = spectrum[:, extent:]
    magnitude = jnp.sqrt(real_part * real_part + imag_part * imag_part)
    smooth = magnitude[:, 0:NBINS]
    for offset in range(1, 2 * HALF + 1):
        smooth = smooth + magnitude[:, offset : offset + NBINS]
    smooth = smooth / (2 * HALF + 1) + 1e-06
    centre_re = real_part[:, HALF : HALF + NBINS] / smooth
    centre_im = imag_part[:, HALF : HALF + NBINS] / smooth
    return jnp.stack([centre_re, centre_im], axis=1).astype(jnp.bfloat16)


def whiten(row_data):
    return normalize(jnp.dot(row_data, band_table(), preferred_element_type=jnp.float32))


SOURCE_BLOCK = 32


def lag_kernel(src_ref, rec_ref, w_ref, o_ref, *, scale):
    real_sum = 0.0
    imag_sum = 0.0
    for window in range(src_ref.shape[0]):
        src = src_ref[window].astype(jnp.float32)[:, None]
        rec = rec_ref[window].astype(jnp.float32)[None]
        real_sum = real_sum + src[:, :, 0] * rec[:, :, 0] + src[:, :, 1] * rec[:, :, 1]
        imag_sum = imag_sum + src[:, :, 1] * rec[:, :, 0] - src[:, :, 0] * rec[:, :, 1]
    lhs = jnp.concatenate([real_sum, imag_sum], axis=2)
    lhs = lhs.reshape(-1, lhs.shape[2]).astype(jnp.bfloat16)
    result = jnp.dot(lhs, w_ref[...], preferred_element_type=jnp.float32) * scale
    o_ref[...] = result.reshape(o_ref.shape)


def cross_transform(sources, receivers, weights, lag_scale):
    windows, count_src = sources.shape[0], sources.shape[1]
    count_rec = receivers.shape[1]
    return pl.pallas_call(
        functools.partial(lag_kernel, scale=lag_scale),
        out_shape=jax.ShapeDtypeStruct((count_src, count_rec, 2 * MAXLAG), jnp.float32),
        grid=(count_src // SOURCE_BLOCK,),
        in_specs=[
            pl.BlockSpec((windows, SOURCE_BLOCK, 2, NBINS), lambda i: (0, i, 0, 0)),
            pl.BlockSpec(receivers.shape, lambda i: (0, 0, 0, 0)),
            pl.BlockSpec(weights.shape, lambda i: (0, 0)),
        ],
        out_specs=pl.BlockSpec((SOURCE_BLOCK, count_rec, 2 * MAXLAG), lambda i: (i, 0, 0)),
    )(sources, receivers, weights)


def ring_gather(value, axis_name, axis):
    size = lax.axis_size(axis_name)
    here = lax.axis_index(axis_name)
    shape = list(value.shape)
    block = shape[axis]
    shape[axis] *= size
    out = jnp.zeros(shape, value.dtype)
    for shift in range(size):
        part = value if shift == 0 else lax.ppermute(
            value, axis_name, [(i, (i + shift) % size) for i in range(size)]
        )
        start = [0] * len(shape)
        start[axis] = ((here - shift) % size) * block
        out = lax.dynamic_update_slice(out, part, start)
    return out


def collect(own):
    part = ring_gather(own, "zh", 0)
    for name in reversed(CHAN_AXES):
        part = ring_gather(part, name, 1)
    return ring_gather(part, "core", 0)


def exchange_receivers(rows):
    here = lax.axis_index(WIN_AXES)
    count = lax.axis_size(WIN_AXES)
    cores = lax.axis_size("core")
    quarter = rows.shape[0] // count
    out = jnp.zeros((count, quarter) + rows.shape[1:], rows.dtype)
    for shift in range(count):
        block = lax.dynamic_slice_in_dim(rows, ((here + shift) % count) * quarter, quarter)
        if shift:
            block = lax.ppermute(block, WIN_AXES, [(i, (i + shift) % count) for i in range(count)])
        origin = (here - shift) % count
        place = (origin % cores) * (count // cores) + origin // cores
        out = lax.dynamic_update_slice(out, block[None], (place, 0, 0, 0))
    return out


def per_device(records, source_rows):
    windows_here, rows_here, samples = records.shape
    whitened = whiten(records.reshape(windows_here * rows_here, samples)).reshape(
        windows_here, rows_here, 2, NBINS
    )
    shards = lax.axis_size(CHAN_AXES)
    block_len = source_rows.shape[1]
    per_shard = block_len // shards
    weights = lag_weights()
    lag_scale = math.sqrt(2.0 / (lax.axis_size(WIN_AXES) * windows_here * NBINS))
    receivers = exchange_receivers(whitened[0])
    shard = lax.axis_index(CHAN_AXES)
    own_rows = lax.dynamic_slice_in_dim(source_rows[0], shard * per_shard, per_shard)
    own_sources = jnp.take(whitened, own_rows, axis=1)
    sources = collect(own_sources)
    return cross_transform(sources, receivers, weights, lag_scale)


def split_mesh(mesh):
    chan, win = mesh.shape["chan"], mesh.shape["win"]
    side = round(chan ** (1 / 3))
    devices = np.asarray(mesh.devices).reshape(side, side, chan // (side * side), win // 2, 2)
    return Mesh(devices, CHAN_AXES + WIN_AXES)


def solution(mesh):
    fine = split_mesh(mesh)
    in_specs = (P(WIN_AXES, CHAN_AXES, None), P())
    out_specs = P(None, CHAN_AXES + WIN_AXES, None)
    return jax.shard_map(
        per_device, mesh=fine, in_specs=in_specs, out_specs=out_specs, check_vma=False
    )
```

```python
import functools
import math

import ml_dtypes
import numpy as np

import jax
import jax.numpy as jnp
from jax import lax
from jax.experimental import pallas as pl
from jax.sharding import Mesh, PartitionSpec as P

S = 7680
NBINS = 512
HALF = 32
FIRST_BIN = 64
MAXLAG = 1024

CHAN_AXES = ("y", "zl", "x")
WIN_AXES = ("zh", "core")


def angle_table(rows, cols):
    turns = np.mod(np.outer(rows.astype(np.int64), cols.astype(np.int64)), S).astype(np.float64)
    angles = turns * (2.0 * np.pi / S)
    return np.cos(angles).astype(np.float32), np.sin(angles).astype(np.float32)


def band_table():
    extent = NBINS + 2 * HALF
    bin_ids = np.arange(FIRST_BIN - HALF, FIRST_BIN - HALF + extent)
    cos, sin = angle_table(np.arange(S), bin_ids)
    table = np.concatenate([cos, -sin], axis=1).astype(ml_dtypes.bfloat16)
    return jnp.asarray(table)


def lag_weights():
    bin_ids = FIRST_BIN + np.arange(NBINS)
    cos, sin = angle_table(bin_ids, np.arange(2 * MAXLAG) - MAXLAG)
    table = np.concatenate([cos, -sin], axis=0).astype(ml_dtypes.bfloat16)
    return jnp.asarray(table)


def normalize(spectrum):
    extent = NBINS + 2 * HALF
    real_part = spectrum[:, :extent]
    imag_part = spectrum[:, extent:]
    magnitude = jnp.sqrt(real_part * real_part + imag_part * imag_part)
    smooth = magnitude[:, 0:NBINS]
    for offset in range(1, 2 * HALF + 1):
        smooth = smooth + magnitude[:, offset : offset + NBINS]
    smooth = smooth / (2 * HALF + 1) + 1e-06
    centre_re = real_part[:, HALF : HALF + NBINS] / smooth
    centre_im = imag_part[:, HALF : HALF + NBINS] / smooth
    return jnp.stack([centre_re, centre_im], axis=1).astype(jnp.bfloat16)


def whiten(row_data):
    return normalize(jnp.dot(row_data, band_table(), preferred_element_type=jnp.float32))


def cross_lhs(sources, receivers):
    src = sources.astype(jnp.float32)[:, :, None]
    rec = receivers.astype(jnp.float32)[:, None]
    real_sum = jnp.sum(src[..., 0, :] * rec[..., 0, :] + src[..., 1, :] * rec[..., 1, :], axis=0)
    imag_sum = jnp.sum(src[..., 1, :] * rec[..., 0, :] - src[..., 0, :] * rec[..., 1, :], axis=0)
    lhs = jnp.concatenate([real_sum, imag_sum], axis=2).reshape(-1, 2 * NBINS)
    return lhs.astype(jnp.bfloat16)


SOURCE_BLOCK = 32


def lag_kernel(lhs_ref, w_ref, o_ref, *, scale):
    result = jnp.dot(lhs_ref[...], w_ref[...], preferred_element_type=jnp.float32) * scale
    o_ref[...] = result.reshape(o_ref.shape)


def transform(lhs, weights, lag_scale, count_rec):
    count_src = lhs.shape[0] // count_rec
    rows = SOURCE_BLOCK * count_rec
    return pl.pallas_call(
        functools.partial(lag_kernel, scale=lag_scale),
        out_shape=jax.ShapeDtypeStruct((count_src, count_rec, 2 * MAXLAG), jnp.float32),
        grid=(count_src // SOURCE_BLOCK,),
        in_specs=[
            pl.BlockSpec((rows, lhs.shape[1]), lambda i: (i, 0)),
            pl.BlockSpec(weights.shape, lambda i: (0, 0)),
        ],
        out_specs=pl.BlockSpec((SOURCE_BLOCK, count_rec, 2 * MAXLAG), lambda i: (i, 0, 0)),
    )(lhs, weights)


def ring_gather(value, axis_name, axis):
    size = lax.axis_size(axis_name)
    here = lax.axis_index(axis_name)
    shape = list(value.shape)
    block = shape[axis]
    shape[axis] *= size
    out = jnp.zeros(shape, value.dtype)
    for shift in range(size):
        part = value if shift == 0 else lax.ppermute(
            value, axis_name, [(i, (i + shift) % size) for i in range(size)]
        )
        start = [0] * len(shape)
        start[axis] = ((here - shift) % size) * block
        out = lax.dynamic_update_slice(out, part, start)
    return out


def swap(value, axis_name):
    return lax.ppermute(value, axis_name, [(0, 1), (1, 0)])


def collect(own, rows):
    zh, core = lax.axis_index("zh"), lax.axis_index("core")
    other_zh, other_core = 1 - zh, 1 - core
    cores = lax.axis_size("core")
    quarter = rows.shape[0] // lax.axis_size(WIN_AXES)

    def rows_of(zh_of, core_of):
        return lax.dynamic_slice_in_dim(rows, (zh_of * cores + core_of) * quarter, quarter)

    from_zh = swap(jnp.stack([rows_of(other_zh, core), rows_of(other_zh, other_core)]), "zh")
    part = ring_gather(own, "zh", 0)
    for name in reversed(CHAN_AXES):
        part = ring_gather(part, name, 1)
    from_core = swap(jnp.stack([rows_of(zh, other_core), from_zh[1]]), "core")
    sources = ring_gather(part, "core", 0)
    receivers = jnp.zeros((cores * lax.axis_size("zh"),) + from_zh.shape[1:], rows.dtype)
    for block, (zh_of, core_of) in (
        (rows_of(zh, core), (zh, core)),
        (from_zh[0], (other_zh, core)),
        (from_core[0], (zh, other_core)),
        (from_core[1], (other_zh, other_core)),
    ):
        place = core_of * lax.axis_size("zh") + zh_of
        receivers = lax.dynamic_update_slice(receivers, block[None], (place, 0, 0, 0))
    return sources, receivers


def per_device(records, source_rows):
    windows_here, rows_here, samples = records.shape
    whitened = whiten(records.reshape(windows_here * rows_here, samples)).reshape(
        windows_here, rows_here, 2, NBINS
    )
    shards = lax.axis_size(CHAN_AXES)
    block_len = source_rows.shape[1]
    per_shard = block_len // shards
    weights = lag_weights()
    lag_scale = math.sqrt(2.0 / (lax.axis_size(WIN_AXES) * windows_here * NBINS))
    shard = lax.axis_index(CHAN_AXES)
    own_rows = lax.dynamic_slice_in_dim(source_rows[0], shard * per_shard, per_shard)
    own_sources = jnp.take(whitened, own_rows, axis=1)
    sources, receivers = collect(own_sources, whitened[0])
    lhs = cross_lhs(sources, receivers)
    return transform(lhs, weights, lag_scale, receivers.shape[1])


def split_mesh(mesh):
    chan, win = mesh.shape["chan"], mesh.shape["win"]
    side = round(chan ** (1 / 3))
    devices = np.asarray(mesh.devices).reshape(side, side, chan // (side * side), win // 2, 2)
    return Mesh(devices, CHAN_AXES + WIN_AXES)


def solution(mesh):
    fine = split_mesh(mesh)
    in_specs = (P(WIN_AXES, CHAN_AXES, None), P())
    out_specs = P(None, CHAN_AXES + WIN_AXES, None)
    return jax.shard_map(
        per_device, mesh=fine, in_specs=in_specs, out_specs=out_specs, check_vma=False
    )
```

```python
import functools
import math

import ml_dtypes
import numpy as np

import jax
import jax.numpy as jnp
from jax import lax
from jax.experimental import pallas as pl
from jax.sharding import Mesh, PartitionSpec as P

S = 7680
NBINS = 512
HALF = 32
FIRST_BIN = 64
MAXLAG = 1024

CHAN_AXES = ("y", "zl", "x")
WIN_AXES = ("zh", "core")


def angle_table(rows, cols):
    turns = np.mod(np.outer(rows.astype(np.int64), cols.astype(np.int64)), S).astype(np.float64)
    angles = turns * (2.0 * np.pi / S)
    return np.cos(angles).astype(np.float32), np.sin(angles).astype(np.float32)


def band_table():
    extent = NBINS + 2 * HALF
    half = S // 2
    rows = (half + 1 + 127) // 128 * 128
    bin_ids = np.arange(FIRST_BIN - HALF, FIRST_BIN - HALF + extent)
    cos, sin = angle_table(np.arange(rows), bin_ids)
    table = np.concatenate([cos, -sin], axis=1)
    table[half + 1 :] = 0.0
    return jnp.asarray(table.astype(ml_dtypes.bfloat16))


def band_spectrum(row_data):
    extent = NBINS + 2 * HALF
    half = S // 2
    table = band_table()
    count = row_data.shape[0]
    pad = table.shape[0] - (half + 1)
    gap = jnp.zeros((count, 1), row_data.dtype)
    head = row_data[:, : half + 1]
    mirror = jnp.concatenate([gap, row_data[:, half + 1 :][:, ::-1], gap], axis=1)
    lhs = jnp.pad(jnp.concatenate([head, mirror], axis=0), ((0, 0), (0, pad)))
    both = jnp.dot(lhs, table, preferred_element_type=jnp.float32)
    real_part = both[:count, :extent] + both[count:, :extent]
    imag_part = both[:count, extent:] - both[count:, extent:]
    return jnp.concatenate([real_part, imag_part], axis=1)


def lag_weights():
    bin_ids = FIRST_BIN + np.arange(NBINS)
    cos, sin = angle_table(bin_ids, np.arange(2 * MAXLAG) - MAXLAG)
    table = np.concatenate([cos, -sin], axis=0).astype(ml_dtypes.bfloat16)
    return jnp.asarray(table)


def normalize(spectrum):
    extent = NBINS + 2 * HALF
    real_part = spectrum[:, :extent]
    imag_part = spectrum[:, extent:]
    magnitude = jnp.sqrt(real_part * real_part + imag_part * imag_part)
    smooth = magnitude[:, 0:NBINS]
    for offset in range(1, 2 * HALF + 1):
        smooth = smooth + magnitude[:, offset : offset + NBINS]
    smooth = smooth / (2 * HALF + 1) + 1e-06
    centre_re = real_part[:, HALF : HALF + NBINS] / smooth
    centre_im = imag_part[:, HALF : HALF + NBINS] / smooth
    return jnp.stack([centre_re, centre_im], axis=1).astype(jnp.bfloat16)


def whiten(row_data):
    return normalize(band_spectrum(row_data))


def cross_lhs(sources, receivers):
    src = sources.astype(jnp.float32)[:, :, None]
    rec = receivers.astype(jnp.float32)[:, None]
    real_sum = jnp.sum(src[..., 0, :] * rec[..., 0, :] + src[..., 1, :] * rec[..., 1, :], axis=0)
    imag_sum = jnp.sum(src[..., 1, :] * rec[..., 0, :] - src[..., 0, :] * rec[..., 1, :], axis=0)
    lhs = jnp.concatenate([real_sum, imag_sum], axis=2).reshape(-1, 2 * NBINS)
    return lhs.astype(jnp.bfloat16)


SOURCE_BLOCK = 32


def lag_kernel(lhs_ref, w_ref, o_ref, *, scale):
    result = jnp.dot(lhs_ref[...], w_ref[...], preferred_element_type=jnp.float32) * scale
    o_ref[...] = result.reshape(o_ref.shape)


def transform(lhs, weights, lag_scale, count_rec):
    count_src = lhs.shape[0] // count_rec
    rows = SOURCE_BLOCK * count_rec
    return pl.pallas_call(
        functools.partial(lag_kernel, scale=lag_scale),
        out_shape=jax.ShapeDtypeStruct((count_src, count_rec, 2 * MAXLAG), jnp.float32),
        grid=(count_src // SOURCE_BLOCK,),
        in_specs=[
            pl.BlockSpec((rows, lhs.shape[1]), lambda i: (i, 0)),
            pl.BlockSpec(weights.shape, lambda i: (0, 0)),
        ],
        out_specs=pl.BlockSpec((SOURCE_BLOCK, count_rec, 2 * MAXLAG), lambda i: (i, 0, 0)),
    )(lhs, weights)


def ring_gather(value, axis_name, axis):
    size = lax.axis_size(axis_name)
    here = lax.axis_index(axis_name)
    shape = list(value.shape)
    block = shape[axis]
    shape[axis] *= size
    out = jnp.zeros(shape, value.dtype)
    for shift in range(size):
        part = value if shift == 0 else lax.ppermute(
            value, axis_name, [(i, (i + shift) % size) for i in range(size)]
        )
        start = [0] * len(shape)
        start[axis] = ((here - shift) % size) * block
        out = lax.dynamic_update_slice(out, part, start)
    return out


def collect(own):
    part = ring_gather(own, "zh", 0)
    for name in reversed(CHAN_AXES):
        part = ring_gather(part, name, 1)
    return ring_gather(part, "core", 0)


def exchange_receivers(rows):
    here = lax.axis_index(WIN_AXES)
    count = lax.axis_size(WIN_AXES)
    cores = lax.axis_size("core")
    quarter = rows.shape[0] // count
    out = jnp.zeros((count, quarter) + rows.shape[1:], rows.dtype)
    for shift in range(count):
        block = lax.dynamic_slice_in_dim(rows, ((here + shift) % count) * quarter, quarter)
        if shift:
            block = lax.ppermute(block, WIN_AXES, [(i, (i + shift) % count) for i in range(count)])
        origin = (here - shift) % count
        place = (origin % cores) * (count // cores) + origin // cores
        out = lax.dynamic_update_slice(out, block[None], (place, 0, 0, 0))
    return out


def per_device(records, source_rows):
    windows_here, rows_here, samples = records.shape
    whitened = whiten(records.reshape(windows_here * rows_here, samples)).reshape(
        windows_here, rows_here, 2, NBINS
    )
    shards = lax.axis_size(CHAN_AXES)
    block_len = source_rows.shape[1]
    per_shard = block_len // shards
    weights = lag_weights()
    lag_scale = math.sqrt(2.0 / (lax.axis_size(WIN_AXES) * windows_here * NBINS))
    receivers = exchange_receivers(whitened[0])
    shard = lax.axis_index(CHAN_AXES)
    own_rows = lax.dynamic_slice_in_dim(source_rows[0], shard * per_shard, per_shard)
    own_sources = jnp.take(whitened, own_rows, axis=1)
    sources = collect(own_sources)
    lhs = cross_lhs(sources, receivers)
    return transform(lhs, weights, lag_scale, receivers.shape[1])


def split_mesh(mesh):
    chan, win = mesh.shape["chan"], mesh.shape["win"]
    side = round(chan ** (1 / 3))
    devices = np.asarray(mesh.devices).reshape(side, side, chan // (side * side), win // 2, 2)
    return Mesh(devices, CHAN_AXES + WIN_AXES)


def solution(mesh):
    fine = split_mesh(mesh)
    in_specs = (P(WIN_AXES, CHAN_AXES, None), P())
    out_specs = P(None, CHAN_AXES + WIN_AXES, None)
    return jax.shard_map(
        per_device, mesh=fine, in_specs=in_specs, out_specs=out_specs, check_vma=False
    )
```

```python
import functools
import math

import ml_dtypes
import numpy as np

import jax
import jax.numpy as jnp
from jax import lax
from jax.experimental import pallas as pl
from jax.sharding import Mesh, PartitionSpec as P

S = 7680
NBINS = 512
HALF = 32
FIRST_BIN = 64
MAXLAG = 1024

CHAN_AXES = ("y", "zl", "x")
WIN_AXES = ("zh", "core")


def angle_table(rows, cols):
    turns = np.mod(np.outer(rows.astype(np.int64), cols.astype(np.int64)), S).astype(np.float64)
    angles = turns * (2.0 * np.pi / S)
    return np.cos(angles).astype(np.float32), np.sin(angles).astype(np.float32)


def band_table():
    extent = NBINS + 2 * HALF
    bin_ids = np.arange(FIRST_BIN - HALF, FIRST_BIN - HALF + extent)
    cos, sin = angle_table(np.arange(S), bin_ids)
    table = np.concatenate([cos, -sin], axis=1).astype(ml_dtypes.bfloat16)
    return jnp.asarray(table)


def lag_weights():
    bin_ids = FIRST_BIN + np.arange(NBINS)
    cos, sin = angle_table(bin_ids, np.arange(2 * MAXLAG) - MAXLAG)
    table = np.concatenate([cos, -sin], axis=0).astype(ml_dtypes.bfloat16)
    return jnp.asarray(table)


def normalize(spectrum):
    extent = NBINS + 2 * HALF
    real_part = spectrum[:, :extent]
    imag_part = spectrum[:, extent:]
    magnitude = jnp.sqrt(real_part * real_part + imag_part * imag_part)
    smooth = magnitude[:, 0:NBINS]
    for offset in range(1, 2 * HALF + 1):
        smooth = smooth + magnitude[:, offset : offset + NBINS]
    smooth = smooth / (2 * HALF + 1) + 1e-06
    centre_re = real_part[:, HALF : HALF + NBINS] / smooth
    centre_im = imag_part[:, HALF : HALF + NBINS] / smooth
    return jnp.stack([centre_re, centre_im], axis=1).astype(jnp.bfloat16)


def whiten(row_data):
    return normalize(jnp.dot(row_data, band_table(), preferred_element_type=jnp.float32))


def cross_lhs(sources, receivers):
    src = sources.astype(jnp.float32)[:, :, None]
    rec = receivers.astype(jnp.float32)[:, None]
    real_sum = jnp.sum(src[..., 0, :] * rec[..., 0, :] + src[..., 1, :] * rec[..., 1, :], axis=0)
    imag_sum = jnp.sum(src[..., 1, :] * rec[..., 0, :] - src[..., 0, :] * rec[..., 1, :], axis=0)
    lhs = jnp.concatenate([real_sum, imag_sum], axis=2).reshape(-1, 2 * NBINS)
    return lhs.astype(jnp.bfloat16)


SOURCE_BLOCK = 64


def lag_kernel(lhs_ref, w_ref, o_ref, *, scale):
    result = jnp.dot(lhs_ref[...], w_ref[...], preferred_element_type=jnp.float32) * scale
    o_ref[...] = result.reshape(o_ref.shape)


def transform(lhs, weights, lag_scale, count_rec):
    count_src = lhs.shape[0] // count_rec
    rows = SOURCE_BLOCK * count_rec
    return pl.pallas_call(
        functools.partial(lag_kernel, scale=lag_scale),
        out_shape=jax.ShapeDtypeStruct((count_src, count_rec, 2 * MAXLAG), jnp.float32),
        grid=(count_src // SOURCE_BLOCK,),
        in_specs=[
            pl.BlockSpec((rows, lhs.shape[1]), lambda i: (i, 0)),
            pl.BlockSpec(weights.shape, lambda i: (0, 0)),
        ],
        out_specs=pl.BlockSpec((SOURCE_BLOCK, count_rec, 2 * MAXLAG), lambda i: (i, 0, 0)),
    )(lhs, weights)


def ring_gather(value, axis_name, axis):
    size = lax.axis_size(axis_name)
    here = lax.axis_index(axis_name)
    shape = list(value.shape)
    block = shape[axis]
    shape[axis] *= size
    out = jnp.zeros(shape, value.dtype)
    for shift in range(size):
        part = value if shift == 0 else lax.ppermute(
            value, axis_name, [(i, (i + shift) % size) for i in range(size)]
        )
        start = [0] * len(shape)
        start[axis] = ((here - shift) % size) * block
        out = lax.dynamic_update_slice(out, part, start)
    return out


def collect(own):
    part = ring_gather(own, "zh", 0)
    for name in reversed(CHAN_AXES):
        part = ring_gather(part, name, 1)
    return ring_gather(part, "core", 0)


def exchange_receivers(rows):
    here = lax.axis_index(WIN_AXES)
    count = lax.axis_size(WIN_AXES)
    cores = lax.axis_size("core")
    quarter = rows.shape[0] // count
    out = jnp.zeros((count, quarter) + rows.shape[1:], rows.dtype)
    for shift in range(count):
        block = lax.dynamic_slice_in_dim(rows, ((here + shift) % count) * quarter, quarter)
        if shift:
            block = lax.ppermute(block, WIN_AXES, [(i, (i + shift) % count) for i in range(count)])
        origin = (here - shift) % count
        place = (origin % cores) * (count // cores) + origin // cores
        out = lax.dynamic_update_slice(out, block[None], (place, 0, 0, 0))
    return out


def per_device(records, source_rows):
    windows_here, rows_here, samples = records.shape
    whitened = whiten(records.reshape(windows_here * rows_here, samples)).reshape(
        windows_here, rows_here, 2, NBINS
    )
    shards = lax.axis_size(CHAN_AXES)
    block_len = source_rows.shape[1]
    per_shard = block_len // shards
    weights = lag_weights()
    lag_scale = math.sqrt(2.0 / (lax.axis_size(WIN_AXES) * windows_here * NBINS))
    receivers = exchange_receivers(whitened[0])
    shard = lax.axis_index(CHAN_AXES)
    own_rows = lax.dynamic_slice_in_dim(source_rows[0], shard * per_shard, per_shard)
    own_sources = jnp.take(whitened, own_rows, axis=1)
    sources = collect(own_sources)
    lhs = cross_lhs(sources, receivers)
    return transform(lhs, weights, lag_scale, receivers.shape[1])


def split_mesh(mesh):
    chan, win = mesh.shape["chan"], mesh.shape["win"]
    side = round(chan ** (1 / 3))
    devices = np.asarray(mesh.devices).reshape(side, side, chan // (side * side), win // 2, 2)
    return Mesh(devices, CHAN_AXES + WIN_AXES)


def solution(mesh):
    fine = split_mesh(mesh)
    in_specs = (P(WIN_AXES, CHAN_AXES, None), P())
    out_specs = P(None, CHAN_AXES + WIN_AXES, None)
    return jax.shard_map(
        per_device, mesh=fine, in_specs=in_specs, out_specs=out_specs, check_vma=False
    )
```

```python
import functools
import math

import ml_dtypes
import numpy as np

import jax
import jax.numpy as jnp
from jax import lax
from jax.experimental import pallas as pl
from jax.sharding import Mesh, PartitionSpec as P

S = 7680
NBINS = 512
HALF = 32
FIRST_BIN = 64
MAXLAG = 1024

CHAN_AXES = ("y", "zl", "x")
WIN_AXES = ("zh", "core")


def angle_table(rows, cols):
    turns = np.mod(np.outer(rows.astype(np.int64), cols.astype(np.int64)), S).astype(np.float64)
    angles = turns * (2.0 * np.pi / S)
    return np.cos(angles).astype(np.float32), np.sin(angles).astype(np.float32)


def band_table():
    extent = NBINS + 2 * HALF
    bin_ids = np.arange(FIRST_BIN - HALF, FIRST_BIN - HALF + extent)
    cos, sin = angle_table(np.arange(S), bin_ids)
    table = np.concatenate([cos, -sin], axis=1).astype(ml_dtypes.bfloat16)
    return jnp.asarray(table)


def lag_weights():
    bin_ids = FIRST_BIN + np.arange(NBINS)
    cos, sin = angle_table(bin_ids, np.arange(2 * MAXLAG) - MAXLAG)
    table = np.concatenate([cos, -sin], axis=0).astype(ml_dtypes.bfloat16)
    return jnp.asarray(table)


def normalize(spectrum):
    extent = NBINS + 2 * HALF
    real_part = spectrum[:, :extent]
    imag_part = spectrum[:, extent:]
    magnitude = jnp.sqrt(real_part * real_part + imag_part * imag_part)
    smooth = magnitude[:, 0:NBINS]
    for offset in range(1, 2 * HALF + 1):
        smooth = smooth + magnitude[:, offset : offset + NBINS]
    smooth = smooth / (2 * HALF + 1) + 1e-06
    centre_re = real_part[:, HALF : HALF + NBINS] / smooth
    centre_im = imag_part[:, HALF : HALF + NBINS] / smooth
    return jnp.stack([centre_re, centre_im], axis=1).astype(jnp.bfloat16)


def whiten(row_data):
    return normalize(jnp.dot(row_data, band_table(), preferred_element_type=jnp.float32))


def cross_lhs(sources, receivers):
    src = sources.astype(jnp.float32)[:, :, None]
    rec = receivers.astype(jnp.float32)[:, None]
    real_sum = jnp.sum(src[..., 0, :] * rec[..., 0, :] + src[..., 1, :] * rec[..., 1, :], axis=0)
    imag_sum = jnp.sum(src[..., 1, :] * rec[..., 0, :] - src[..., 0, :] * rec[..., 1, :], axis=0)
    lhs = jnp.concatenate([real_sum, imag_sum], axis=2).reshape(-1, 2 * NBINS)
    return lhs.astype(jnp.bfloat16)


SOURCE_BLOCK = 128


def lag_kernel(lhs_ref, w_ref, o_ref, *, scale):
    result = jnp.dot(lhs_ref[...], w_ref[...], preferred_element_type=jnp.float32) * scale
    o_ref[...] = result.reshape(o_ref.shape)


def transform(lhs, weights, lag_scale, count_rec):
    count_src = lhs.shape[0] // count_rec
    rows = SOURCE_BLOCK * count_rec
    return pl.pallas_call(
        functools.partial(lag_kernel, scale=lag_scale),
        out_shape=jax.ShapeDtypeStruct((count_src, count_rec, 2 * MAXLAG), jnp.float32),
        grid=(count_src // SOURCE_BLOCK,),
        in_specs=[
            pl.BlockSpec((rows, lhs.shape[1]), lambda i: (i, 0)),
            pl.BlockSpec(weights.shape, lambda i: (0, 0)),
        ],
        out_specs=pl.BlockSpec((SOURCE_BLOCK, count_rec, 2 * MAXLAG), lambda i: (i, 0, 0)),
    )(lhs, weights)


def ring_gather(value, axis_name, axis):
    size = lax.axis_size(axis_name)
    here = lax.axis_index(axis_name)
    shape = list(value.shape)
    block = shape[axis]
    shape[axis] *= size
    out = jnp.zeros(shape, value.dtype)
    for shift in range(size):
        part = value if shift == 0 else lax.ppermute(
            value, axis_name, [(i, (i + shift) % size) for i in range(size)]
        )
        start = [0] * len(shape)
        start[axis] = ((here - shift) % size) * block
        out = lax.dynamic_update_slice(out, part, start)
    return out


def collect(own):
    part = ring_gather(own, "zh", 0)
    for name in reversed(CHAN_AXES):
        part = ring_gather(part, name, 1)
    return ring_gather(part, "core", 0)


def exchange_receivers(rows):
    here = lax.axis_index(WIN_AXES)
    count = lax.axis_size(WIN_AXES)
    cores = lax.axis_size("core")
    quarter = rows.shape[0] // count
    out = jnp.zeros((count, quarter) + rows.shape[1:], rows.dtype)
    for shift in range(count):
        block = lax.dynamic_slice_in_dim(rows, ((here + shift) % count) * quarter, quarter)
        if shift:
            block = lax.ppermute(block, WIN_AXES, [(i, (i + shift) % count) for i in range(count)])
        origin = (here - shift) % count
        place = (origin % cores) * (count // cores) + origin // cores
        out = lax.dynamic_update_slice(out, block[None], (place, 0, 0, 0))
    return out


def per_device(records, source_rows):
    windows_here, rows_here, samples = records.shape
    whitened = whiten(records.reshape(windows_here * rows_here, samples)).reshape(
        windows_here, rows_here, 2, NBINS
    )
    shards = lax.axis_size(CHAN_AXES)
    block_len = source_rows.shape[1]
    per_shard = block_len // shards
    weights = lag_weights()
    lag_scale = math.sqrt(2.0 / (lax.axis_size(WIN_AXES) * windows_here * NBINS))
    receivers = exchange_receivers(whitened[0])
    shard = lax.axis_index(CHAN_AXES)
    own_rows = lax.dynamic_slice_in_dim(source_rows[0], shard * per_shard, per_shard)
    own_sources = jnp.take(whitened, own_rows, axis=1)
    sources = collect(own_sources)
    lhs = cross_lhs(sources, receivers)
    return transform(lhs, weights, lag_scale, receivers.shape[1])


def split_mesh(mesh):
    chan, win = mesh.shape["chan"], mesh.shape["win"]
    side = round(chan ** (1 / 3))
    devices = np.asarray(mesh.devices).reshape(side, side, chan // (side * side), win // 2, 2)
    return Mesh(devices, CHAN_AXES + WIN_AXES)


def solution(mesh):
    fine = split_mesh(mesh)
    in_specs = (P(WIN_AXES, CHAN_AXES, None), P())
    out_specs = P(None, CHAN_AXES + WIN_AXES, None)
    return jax.shard_map(
        per_device, mesh=fine, in_specs=in_specs, out_specs=out_specs, check_vma=False
    )
```

```python
import functools
import math

import ml_dtypes
import numpy as np

import jax
import jax.numpy as jnp
from jax import lax
from jax.experimental import pallas as pl
from jax.sharding import Mesh, PartitionSpec as P

S = 7680
NBINS = 512
HALF = 32
FIRST_BIN = 64
MAXLAG = 1024

CHAN_AXES = ("y", "zl", "x")
WIN_AXES = ("zh", "core")


def angle_table(rows, cols):
    turns = np.mod(np.outer(rows.astype(np.int64), cols.astype(np.int64)), S).astype(np.float64)
    angles = turns * (2.0 * np.pi / S)
    return np.cos(angles).astype(np.float32), np.sin(angles).astype(np.float32)


def band_table():
    extent = NBINS + 2 * HALF
    bin_ids = np.arange(FIRST_BIN - HALF, FIRST_BIN - HALF + extent)
    cos, sin = angle_table(np.arange(S), bin_ids)
    table = np.concatenate([cos, -sin], axis=1).astype(ml_dtypes.bfloat16)
    return jnp.asarray(table)


def lag_weights():
    bin_ids = FIRST_BIN + np.arange(NBINS)
    cos, sin = angle_table(bin_ids, np.arange(2 * MAXLAG) - MAXLAG)
    table = np.concatenate([cos, -sin], axis=0).astype(ml_dtypes.bfloat16)
    return jnp.asarray(table)


def normalize(spectrum):
    extent = NBINS + 2 * HALF
    real_part = spectrum[:, :extent]
    imag_part = spectrum[:, extent:]
    magnitude = jnp.sqrt(real_part * real_part + imag_part * imag_part)
    smooth = magnitude[:, 0:NBINS]
    for offset in range(1, 2 * HALF + 1):
        smooth = smooth + magnitude[:, offset : offset + NBINS]
    smooth = smooth / (2 * HALF + 1) + 1e-06
    centre_re = real_part[:, HALF : HALF + NBINS] / smooth
    centre_im = imag_part[:, HALF : HALF + NBINS] / smooth
    return jnp.stack([centre_re, centre_im], axis=1).astype(jnp.bfloat16)


def whiten(row_data):
    return normalize(jnp.dot(row_data, band_table(), preferred_element_type=jnp.float32))


def cross_parts(sources, receivers):
    src = sources.astype(jnp.float32)[:, :, None]
    rec = receivers.astype(jnp.float32)[:, None]
    real_sum = jnp.sum(src[..., 0, :] * rec[..., 0, :] + src[..., 1, :] * rec[..., 1, :], axis=0)
    imag_sum = jnp.sum(src[..., 1, :] * rec[..., 0, :] - src[..., 0, :] * rec[..., 1, :], axis=0)
    return real_sum.astype(jnp.bfloat16), imag_sum.astype(jnp.bfloat16)


SOURCE_BLOCK = 64


def lag_kernel(re_ref, im_ref, w_ref, o_ref, *, scale):
    def flat(ref):
        return ref[...].astype(jnp.float32).reshape(-1, ref.shape[2]).astype(jnp.bfloat16)

    bins = re_ref.shape[2]
    result = jnp.dot(flat(re_ref), w_ref[:bins], preferred_element_type=jnp.float32)
    result = result + jnp.dot(flat(im_ref), w_ref[bins:], preferred_element_type=jnp.float32)
    o_ref[...] = (result * scale).reshape(o_ref.shape)


def transform(real_part, imag_part, weights, lag_scale):
    count_src, count_rec, bins = real_part.shape
    part_spec = pl.BlockSpec((SOURCE_BLOCK, count_rec, bins), lambda i: (i, 0, 0))
    return pl.pallas_call(
        functools.partial(lag_kernel, scale=lag_scale),
        out_shape=jax.ShapeDtypeStruct((count_src, count_rec, 2 * MAXLAG), jnp.float32),
        grid=(count_src // SOURCE_BLOCK,),
        in_specs=[part_spec, part_spec, pl.BlockSpec(weights.shape, lambda i: (0, 0))],
        out_specs=pl.BlockSpec((SOURCE_BLOCK, count_rec, 2 * MAXLAG), lambda i: (i, 0, 0)),
    )(real_part, imag_part, weights)


def ring_gather(value, axis_name, axis):
    size = lax.axis_size(axis_name)
    here = lax.axis_index(axis_name)
    shape = list(value.shape)
    block = shape[axis]
    shape[axis] *= size
    out = jnp.zeros(shape, value.dtype)
    for shift in range(size):
        part = value if shift == 0 else lax.ppermute(
            value, axis_name, [(i, (i + shift) % size) for i in range(size)]
        )
        start = [0] * len(shape)
        start[axis] = ((here - shift) % size) * block
        out = lax.dynamic_update_slice(out, part, start)
    return out


def collect(own):
    part = ring_gather(own, "zh", 0)
    for name in reversed(CHAN_AXES):
        part = ring_gather(part, name, 1)
    return ring_gather(part, "core", 0)


def exchange_receivers(rows):
    here = lax.axis_index(WIN_AXES)
    count = lax.axis_size(WIN_AXES)
    cores = lax.axis_size("core")
    quarter = rows.shape[0] // count
    out = jnp.zeros((count, quarter) + rows.shape[1:], rows.dtype)
    for shift in range(count):
        block = lax.dynamic_slice_in_dim(rows, ((here + shift) % count) * quarter, quarter)
        if shift:
            block = lax.ppermute(block, WIN_AXES, [(i, (i + shift) % count) for i in range(count)])
        origin = (here - shift) % count
        place = (origin % cores) * (count // cores) + origin // cores
        out = lax.dynamic_update_slice(out, block[None], (place, 0, 0, 0))
    return out


def per_device(records, source_rows):
    windows_here, rows_here, samples = records.shape
    whitened = whiten(records.reshape(windows_here * rows_here, samples)).reshape(
        windows_here, rows_here, 2, NBINS
    )
    shards = lax.axis_size(CHAN_AXES)
    block_len = source_rows.shape[1]
    per_shard = block_len // shards
    weights = lag_weights()
    lag_scale = math.sqrt(2.0 / (lax.axis_size(WIN_AXES) * windows_here * NBINS))
    receivers = exchange_receivers(whitened[0])
    shard = lax.axis_index(CHAN_AXES)
    own_rows = lax.dynamic_slice_in_dim(source_rows[0], shard * per_shard, per_shard)
    own_sources = jnp.take(whitened, own_rows, axis=1)
    sources = collect(own_sources)
    real_part, imag_part = cross_parts(sources, receivers)
    return transform(real_part, imag_part, weights, lag_scale)


def split_mesh(mesh):
    chan, win = mesh.shape["chan"], mesh.shape["win"]
    side = round(chan ** (1 / 3))
    devices = np.asarray(mesh.devices).reshape(side, side, chan // (side * side), win // 2, 2)
    return Mesh(devices, CHAN_AXES + WIN_AXES)


def solution(mesh):
    fine = split_mesh(mesh)
    in_specs = (P(WIN_AXES, CHAN_AXES, None), P())
    out_specs = P(None, CHAN_AXES + WIN_AXES, None)
    return jax.shard_map(
        per_device, mesh=fine, in_specs=in_specs, out_specs=out_specs, check_vma=False
    )
```

```python
import functools
import math

import ml_dtypes
import numpy as np

import jax
import jax.numpy as jnp
from jax import lax
from jax.experimental import pallas as pl
from jax.sharding import Mesh, PartitionSpec as P

S = 7680
NBINS = 512
HALF = 32
FIRST_BIN = 64
MAXLAG = 1024

CHAN_AXES = ("y", "zl", "x")
WIN_AXES = ("zh", "core")


def angle_table(rows, cols):
    turns = np.mod(np.outer(rows.astype(np.int64), cols.astype(np.int64)), S).astype(np.float64)
    angles = turns * (2.0 * np.pi / S)
    return np.cos(angles).astype(np.float32), np.sin(angles).astype(np.float32)


def band_table():
    extent = NBINS + 2 * HALF
    bin_ids = np.arange(FIRST_BIN - HALF, FIRST_BIN - HALF + extent)
    cos, sin = angle_table(np.arange(S), bin_ids)
    table = np.concatenate([cos, -sin], axis=1).astype(ml_dtypes.bfloat16)
    return jnp.asarray(table)


def lag_weights():
    bin_ids = FIRST_BIN + np.arange(NBINS)
    cos, sin = angle_table(bin_ids, np.arange(2 * MAXLAG) - MAXLAG)
    table = np.concatenate([cos, -sin], axis=0).astype(ml_dtypes.bfloat16)
    return jnp.asarray(table)


def normalize(spectrum):
    extent = NBINS + 2 * HALF
    real_part = spectrum[:, :extent]
    imag_part = spectrum[:, extent:]
    magnitude = jnp.sqrt(real_part * real_part + imag_part * imag_part)
    smooth = magnitude[:, 0:NBINS]
    for offset in range(1, 2 * HALF + 1):
        smooth = smooth + magnitude[:, offset : offset + NBINS]
    smooth = smooth / (2 * HALF + 1) + 1e-06
    centre_re = real_part[:, HALF : HALF + NBINS] / smooth
    centre_im = imag_part[:, HALF : HALF + NBINS] / smooth
    return jnp.stack([centre_re, centre_im], axis=1).astype(jnp.bfloat16)


def whiten(row_data):
    return normalize(jnp.dot(row_data, band_table(), preferred_element_type=jnp.float32))


def cross_parts(sources, receivers):
    src = sources.astype(jnp.float32)[:, :, None]
    rec = receivers.astype(jnp.float32)[:, None]
    real_sum = jnp.sum(src[..., 0, :] * rec[..., 0, :] + src[..., 1, :] * rec[..., 1, :], axis=0)
    imag_sum = jnp.sum(src[..., 1, :] * rec[..., 0, :] - src[..., 0, :] * rec[..., 1, :], axis=0)
    return real_sum.astype(jnp.bfloat16), imag_sum.astype(jnp.bfloat16)


SOURCE_BLOCK = 64


def lag_kernel(re_ref, im_ref, w_ref, o_ref, *, scale):
    count_rec, block, bins = re_ref.shape
    result = jnp.dot(re_ref[...].reshape(-1, bins), w_ref[:bins], preferred_element_type=jnp.float32)
    result = result + jnp.dot(im_ref[...].reshape(-1, bins), w_ref[bins:], preferred_element_type=jnp.float32)
    result = (result * scale).reshape(count_rec, block, result.shape[1])
    o_ref[...] = jnp.swapaxes(result, 0, 1)


def transform(real_part, imag_part, weights, lag_scale):
    count_src, count_rec, bins = real_part.shape
    part_spec = pl.BlockSpec((count_rec, SOURCE_BLOCK, bins), lambda i: (0, i, 0))
    return pl.pallas_call(
        functools.partial(lag_kernel, scale=lag_scale),
        out_shape=jax.ShapeDtypeStruct((count_src, count_rec, 2 * MAXLAG), jnp.float32),
        grid=(count_src // SOURCE_BLOCK,),
        in_specs=[part_spec, part_spec, pl.BlockSpec(weights.shape, lambda i: (0, 0))],
        out_specs=pl.BlockSpec((SOURCE_BLOCK, count_rec, 2 * MAXLAG), lambda i: (i, 0, 0)),
    )(jnp.swapaxes(real_part, 0, 1), jnp.swapaxes(imag_part, 0, 1), weights)


def ring_gather(value, axis_name, axis):
    size = lax.axis_size(axis_name)
    here = lax.axis_index(axis_name)
    shape = list(value.shape)
    block = shape[axis]
    shape[axis] *= size
    out = jnp.zeros(shape, value.dtype)
    for shift in range(size):
        part = value if shift == 0 else lax.ppermute(
            value, axis_name, [(i, (i + shift) % size) for i in range(size)]
        )
        start = [0] * len(shape)
        start[axis] = ((here - shift) % size) * block
        out = lax.dynamic_update_slice(out, part, start)
    return out


def collect(own):
    part = ring_gather(own, "zh", 0)
    for name in reversed(CHAN_AXES):
        part = ring_gather(part, name, 1)
    return ring_gather(part, "core", 0)


def exchange_receivers(rows):
    here = lax.axis_index(WIN_AXES)
    count = lax.axis_size(WIN_AXES)
    cores = lax.axis_size("core")
    quarter = rows.shape[0] // count
    out = jnp.zeros((count, quarter) + rows.shape[1:], rows.dtype)
    for shift in range(count):
        block = lax.dynamic_slice_in_dim(rows, ((here + shift) % count) * quarter, quarter)
        if shift:
            block = lax.ppermute(block, WIN_AXES, [(i, (i + shift) % count) for i in range(count)])
        origin = (here - shift) % count
        place = (origin % cores) * (count // cores) + origin // cores
        out = lax.dynamic_update_slice(out, block[None], (place, 0, 0, 0))
    return out


def per_device(records, source_rows):
    windows_here, rows_here, samples = records.shape
    whitened = whiten(records.reshape(windows_here * rows_here, samples)).reshape(
        windows_here, rows_here, 2, NBINS
    )
    shards = lax.axis_size(CHAN_AXES)
    block_len = source_rows.shape[1]
    per_shard = block_len // shards
    weights = lag_weights()
    lag_scale = math.sqrt(2.0 / (lax.axis_size(WIN_AXES) * windows_here * NBINS))
    receivers = exchange_receivers(whitened[0])
    shard = lax.axis_index(CHAN_AXES)
    own_rows = lax.dynamic_slice_in_dim(source_rows[0], shard * per_shard, per_shard)
    own_sources = jnp.take(whitened, own_rows, axis=1)
    sources = collect(own_sources)
    real_part, imag_part = cross_parts(sources, receivers)
    return transform(real_part, imag_part, weights, lag_scale)


def split_mesh(mesh):
    chan, win = mesh.shape["chan"], mesh.shape["win"]
    side = round(chan ** (1 / 3))
    devices = np.asarray(mesh.devices).reshape(side, side, chan // (side * side), win // 2, 2)
    return Mesh(devices, CHAN_AXES + WIN_AXES)


def solution(mesh):
    fine = split_mesh(mesh)
    in_specs = (P(WIN_AXES, CHAN_AXES, None), P())
    out_specs = P(None, CHAN_AXES + WIN_AXES, None)
    return jax.shard_map(
        per_device, mesh=fine, in_specs=in_specs, out_specs=out_specs, check_vma=False
    )
```

```python
import functools
import math

import ml_dtypes
import numpy as np

import jax
import jax.numpy as jnp
from jax import lax
from jax.experimental import pallas as pl
from jax.sharding import Mesh, PartitionSpec as P

S = 7680
NBINS = 512
HALF = 32
FIRST_BIN = 64
MAXLAG = 1024

CHAN_AXES = ("y", "zl", "x")
WIN_AXES = ("zh", "core")


def angle_table(rows, cols):
    turns = np.mod(np.outer(rows.astype(np.int64), cols.astype(np.int64)), S).astype(np.float64)
    angles = turns * (2.0 * np.pi / S)
    return np.cos(angles).astype(np.float32), np.sin(angles).astype(np.float32)


def band_table():
    extent = NBINS + 2 * HALF
    bin_ids = np.arange(FIRST_BIN - HALF, FIRST_BIN - HALF + extent)
    cos, sin = angle_table(np.arange(S), bin_ids)
    table = np.concatenate([cos, -sin], axis=1).astype(ml_dtypes.bfloat16)
    return jnp.asarray(table)


def lag_weights():
    bin_ids = FIRST_BIN + np.arange(NBINS)
    cos, sin = angle_table(bin_ids, np.arange(2 * MAXLAG) - MAXLAG)
    table = np.concatenate([cos, -sin], axis=0).astype(ml_dtypes.bfloat16)
    return jnp.asarray(table)


def normalize(spectrum):
    extent = NBINS + 2 * HALF
    real_part = spectrum[:, :extent]
    imag_part = spectrum[:, extent:]
    magnitude = jnp.sqrt(real_part * real_part + imag_part * imag_part)
    smooth = magnitude[:, 0:NBINS]
    for offset in range(1, 2 * HALF + 1):
        smooth = smooth + magnitude[:, offset : offset + NBINS]
    smooth = smooth / (2 * HALF + 1) + 1e-06
    centre_re = real_part[:, HALF : HALF + NBINS] / smooth
    centre_im = imag_part[:, HALF : HALF + NBINS] / smooth
    return jnp.stack([centre_re, centre_im], axis=1).astype(jnp.bfloat16)


def whiten(row_data):
    return normalize(jnp.dot(row_data, band_table(), preferred_element_type=jnp.float32))


def cross_parts(sources, receivers):
    src = sources.astype(jnp.float32)[:, :, None]
    rec = receivers.astype(jnp.float32)[:, None]
    real_sum = jnp.sum(src[..., 0, :] * rec[..., 0, :] + src[..., 1, :] * rec[..., 1, :], axis=0)
    imag_sum = jnp.sum(src[..., 1, :] * rec[..., 0, :] - src[..., 0, :] * rec[..., 1, :], axis=0)
    return real_sum.astype(jnp.bfloat16), imag_sum.astype(jnp.bfloat16)


SOURCE_BLOCK = 64


def lag_kernel(re_ref, im_ref, w_ref, o_ref, *, scale):
    count_rec, block, bins = re_ref.shape
    result = jnp.dot(re_ref[...].reshape(-1, bins), w_ref[:bins], preferred_element_type=jnp.float32)
    result = result + jnp.dot(im_ref[...].reshape(-1, bins), w_ref[bins:], preferred_element_type=jnp.float32)
    result = (result * scale).reshape(count_rec, block, result.shape[1])
    o_ref[...] = jnp.swapaxes(result, 0, 1)


def transform(real_part, imag_part, weights, lag_scale):
    count_src, count_rec, bins = real_part.shape
    part_spec = pl.BlockSpec((count_rec, SOURCE_BLOCK, bins), lambda i: (0, i, 0))
    return pl.pallas_call(
        functools.partial(lag_kernel, scale=lag_scale),
        out_shape=jax.ShapeDtypeStruct((count_src, count_rec, 2 * MAXLAG), jnp.float32),
        grid=(count_src // SOURCE_BLOCK,),
        in_specs=[part_spec, part_spec, pl.BlockSpec(weights.shape, lambda i: (0, 0))],
        out_specs=pl.BlockSpec((SOURCE_BLOCK, count_rec, 2 * MAXLAG), lambda i: (i, 0, 0)),
    )(jnp.swapaxes(real_part, 0, 1), jnp.swapaxes(imag_part, 0, 1), weights)


def ring_gather(value, axis_name, axis):
    size = lax.axis_size(axis_name)
    here = lax.axis_index(axis_name)
    shape = list(value.shape)
    block = shape[axis]
    shape[axis] *= size
    out = jnp.zeros(shape, value.dtype)
    for shift in range(size):
        part = value if shift == 0 else lax.ppermute(
            value, axis_name, [(i, (i + shift) % size) for i in range(size)]
        )
        start = [0] * len(shape)
        start[axis] = ((here - shift) % size) * block
        out = lax.dynamic_update_slice(out, part, start)
    return out


def collect(own):
    part = ring_gather(own, "zh", 0)
    for name in reversed(CHAN_AXES):
        part = ring_gather(part, name, 1)
    return ring_gather(part, "core", 0)


def exchange_receivers(rows):
    here = lax.axis_index(WIN_AXES)
    count = lax.axis_size(WIN_AXES)
    cores = lax.axis_size("core")
    quarter = rows.shape[0] // count
    out = jnp.zeros((count, quarter) + rows.shape[1:], rows.dtype)
    for shift in range(count):
        block = lax.dynamic_slice_in_dim(rows, ((here + shift) % count) * quarter, quarter)
        if shift:
            block = lax.ppermute(block, WIN_AXES, [(i, (i + shift) % count) for i in range(count)])
        origin = (here - shift) % count
        place = (origin % cores) * (count // cores) + origin // cores
        out = lax.dynamic_update_slice(out, block[None], (place, 0, 0, 0))
    return out


def per_device(records, source_rows):
    windows_here, rows_here, samples = records.shape
    whitened = whiten(records.reshape(windows_here * rows_here, samples)).reshape(
        windows_here, rows_here, 2, NBINS
    )
    shards = lax.axis_size(CHAN_AXES)
    block_len = source_rows.shape[1]
    per_shard = block_len // shards
    weights = lag_weights()
    lag_scale = math.sqrt(2.0 / (lax.axis_size(WIN_AXES) * windows_here * NBINS))
    receivers = exchange_receivers(whitened[0])
    shard = lax.axis_index(CHAN_AXES)
    own_rows = lax.dynamic_slice_in_dim(source_rows[0], shard * per_shard, per_shard)
    own_records = jnp.take(records[0], own_rows, axis=0)
    own_sources = whiten(own_records).reshape(1, per_shard, 2, NBINS)
    sources = collect(own_sources)
    real_part, imag_part = cross_parts(sources, receivers)
    return transform(real_part, imag_part, weights, lag_scale)


def split_mesh(mesh):
    chan, win = mesh.shape["chan"], mesh.shape["win"]
    side = round(chan ** (1 / 3))
    devices = np.asarray(mesh.devices).reshape(side, side, chan // (side * side), win // 2, 2)
    return Mesh(devices, CHAN_AXES + WIN_AXES)


def solution(mesh):
    fine = split_mesh(mesh)
    in_specs = (P(WIN_AXES, CHAN_AXES, None), P())
    out_specs = P(None, CHAN_AXES + WIN_AXES, None)
    return jax.shard_map(
        per_device, mesh=fine, in_specs=in_specs, out_specs=out_specs, check_vma=False
    )
```

```python
import functools
import math

import ml_dtypes
import numpy as np

import jax
import jax.numpy as jnp
from jax import lax
from jax.experimental import pallas as pl
from jax.sharding import Mesh, PartitionSpec as P

S = 7680
NBINS = 512
HALF = 32
FIRST_BIN = 64
MAXLAG = 1024

CHAN_AXES = ("y", "zl", "x")
WIN_AXES = ("zh", "core")


def angle_table(rows, cols):
    turns = np.mod(np.outer(rows.astype(np.int64), cols.astype(np.int64)), S).astype(np.float64)
    angles = turns * (2.0 * np.pi / S)
    return np.cos(angles).astype(np.float32), np.sin(angles).astype(np.float32)


def band_table():
    extent = NBINS + 2 * HALF
    bin_ids = np.arange(FIRST_BIN - HALF, FIRST_BIN - HALF + extent)
    cos, sin = angle_table(np.arange(S), bin_ids)
    table = np.concatenate([cos, -sin], axis=1).astype(ml_dtypes.bfloat16)
    return jnp.asarray(table)


def lag_weights():
    bin_ids = FIRST_BIN + np.arange(NBINS)
    cos, sin = angle_table(bin_ids, np.arange(2 * MAXLAG) - MAXLAG)
    table = np.concatenate([cos, -sin], axis=0).astype(ml_dtypes.bfloat16)
    return jnp.asarray(table)


def normalize(spectrum):
    extent = NBINS + 2 * HALF
    real_part = spectrum[:, :extent]
    imag_part = spectrum[:, extent:]
    magnitude = jnp.sqrt(real_part * real_part + imag_part * imag_part)
    smooth = magnitude[:, 0:NBINS]
    for offset in range(1, 2 * HALF + 1):
        smooth = smooth + magnitude[:, offset : offset + NBINS]
    smooth = smooth / (2 * HALF + 1) + 1e-06
    centre_re = real_part[:, HALF : HALF + NBINS] / smooth
    centre_im = imag_part[:, HALF : HALF + NBINS] / smooth
    return jnp.stack([centre_re, centre_im], axis=1).astype(jnp.bfloat16)


def whiten(row_data):
    return normalize(jnp.dot(row_data, band_table(), preferred_element_type=jnp.float32))


def cross_parts(sources, receivers):
    src = sources.astype(jnp.float32)[:, :, None]
    rec = receivers.astype(jnp.float32)[:, None]
    real_sum = jnp.sum(src[..., 0, :] * rec[..., 0, :] + src[..., 1, :] * rec[..., 1, :], axis=0)
    imag_sum = jnp.sum(src[..., 1, :] * rec[..., 0, :] - src[..., 0, :] * rec[..., 1, :], axis=0)
    return real_sum.astype(jnp.bfloat16), imag_sum.astype(jnp.bfloat16)


SOURCE_BLOCK = 128


def lag_kernel(re_ref, im_ref, w_ref, o_ref, *, scale):
    count_rec, block, bins = re_ref.shape
    result = jnp.dot(re_ref[...].reshape(-1, bins), w_ref[:bins], preferred_element_type=jnp.float32)
    result = result + jnp.dot(im_ref[...].reshape(-1, bins), w_ref[bins:], preferred_element_type=jnp.float32)
    result = (result * scale).reshape(count_rec, block, result.shape[1])
    o_ref[...] = jnp.swapaxes(result, 0, 1)


def transform(real_part, imag_part, weights, lag_scale):
    count_src, count_rec, bins = real_part.shape
    part_spec = pl.BlockSpec((count_rec, SOURCE_BLOCK, bins), lambda i: (0, i, 0))
    return pl.pallas_call(
        functools.partial(lag_kernel, scale=lag_scale),
        out_shape=jax.ShapeDtypeStruct((count_src, count_rec, 2 * MAXLAG), jnp.float32),
        grid=(count_src // SOURCE_BLOCK,),
        in_specs=[part_spec, part_spec, pl.BlockSpec(weights.shape, lambda i: (0, 0))],
        out_specs=pl.BlockSpec((SOURCE_BLOCK, count_rec, 2 * MAXLAG), lambda i: (i, 0, 0)),
    )(jnp.swapaxes(real_part, 0, 1), jnp.swapaxes(imag_part, 0, 1), weights)


def ring_gather(value, axis_name, axis):
    size = lax.axis_size(axis_name)
    here = lax.axis_index(axis_name)
    shape = list(value.shape)
    block = shape[axis]
    shape[axis] *= size
    out = jnp.zeros(shape, value.dtype)
    for shift in range(size):
        part = value if shift == 0 else lax.ppermute(
            value, axis_name, [(i, (i + shift) % size) for i in range(size)]
        )
        start = [0] * len(shape)
        start[axis] = ((here - shift) % size) * block
        out = lax.dynamic_update_slice(out, part, start)
    return out


def collect(own):
    part = ring_gather(own, "zh", 0)
    for name in reversed(CHAN_AXES):
        part = ring_gather(part, name, 1)
    return ring_gather(part, "core", 0)


def exchange_receivers(rows):
    here = lax.axis_index(WIN_AXES)
    count = lax.axis_size(WIN_AXES)
    cores = lax.axis_size("core")
    quarter = rows.shape[0] // count
    out = jnp.zeros((count, quarter) + rows.shape[1:], rows.dtype)
    for shift in range(count):
        block = lax.dynamic_slice_in_dim(rows, ((here + shift) % count) * quarter, quarter)
        if shift:
            block = lax.ppermute(block, WIN_AXES, [(i, (i + shift) % count) for i in range(count)])
        origin = (here - shift) % count
        place = (origin % cores) * (count // cores) + origin // cores
        out = lax.dynamic_update_slice(out, block[None], (place, 0, 0, 0))
    return out


def per_device(records, source_rows):
    windows_here, rows_here, samples = records.shape
    whitened = whiten(records.reshape(windows_here * rows_here, samples)).reshape(
        windows_here, rows_here, 2, NBINS
    )
    shards = lax.axis_size(CHAN_AXES)
    block_len = source_rows.shape[1]
    per_shard = block_len // shards
    weights = lag_weights()
    lag_scale = math.sqrt(2.0 / (lax.axis_size(WIN_AXES) * windows_here * NBINS))
    receivers = exchange_receivers(whitened[0])
    shard = lax.axis_index(CHAN_AXES)
    own_rows = lax.dynamic_slice_in_dim(source_rows[0], shard * per_shard, per_shard)
    own_sources = jnp.take(whitened, own_rows, axis=1)
    sources = collect(own_sources)
    real_part, imag_part = cross_parts(sources, receivers)
    return transform(real_part, imag_part, weights, lag_scale)


def split_mesh(mesh):
    chan, win = mesh.shape["chan"], mesh.shape["win"]
    side = round(chan ** (1 / 3))
    devices = np.asarray(mesh.devices).reshape(side, side, chan // (side * side), win // 2, 2)
    return Mesh(devices, CHAN_AXES + WIN_AXES)


def solution(mesh):
    fine = split_mesh(mesh)
    in_specs = (P(WIN_AXES, CHAN_AXES, None), P())
    out_specs = P(None, CHAN_AXES + WIN_AXES, None)
    return jax.shard_map(
        per_device, mesh=fine, in_specs=in_specs, out_specs=out_specs, check_vma=False
    )
```

```python
import functools
import math

import ml_dtypes
import numpy as np

import jax
import jax.numpy as jnp
from jax import lax
from jax.experimental import pallas as pl
from jax.sharding import Mesh, PartitionSpec as P

S = 7680
NBINS = 512
HALF = 32
FIRST_BIN = 64
MAXLAG = 1024

CHAN_AXES = ("y", "zl", "x")
WIN_AXES = ("zh", "core")


def angle_table(rows, cols):
    turns = np.mod(np.outer(rows.astype(np.int64), cols.astype(np.int64)), S).astype(np.float64)
    angles = turns * (2.0 * np.pi / S)
    return np.cos(angles).astype(np.float32), np.sin(angles).astype(np.float32)


def band_table():
    extent = NBINS + 2 * HALF
    bin_ids = np.arange(FIRST_BIN - HALF, FIRST_BIN - HALF + extent)
    cos, sin = angle_table(np.arange(S), bin_ids)
    table = np.concatenate([cos, -sin], axis=1).astype(ml_dtypes.bfloat16)
    return jnp.asarray(table)


def lag_weights():
    bin_ids = FIRST_BIN + np.arange(NBINS)
    cos, sin = angle_table(bin_ids, np.arange(2 * MAXLAG) - MAXLAG)
    table = np.concatenate([cos, -sin], axis=0).astype(ml_dtypes.bfloat16)
    return jnp.asarray(table)


def normalize(spectrum):
    extent = NBINS + 2 * HALF
    real_part = spectrum[:, :extent]
    imag_part = spectrum[:, extent:]
    magnitude = jnp.sqrt(real_part * real_part + imag_part * imag_part)
    smooth = magnitude[:, 0:NBINS]
    for offset in range(1, 2 * HALF + 1):
        smooth = smooth + magnitude[:, offset : offset + NBINS]
    smooth = smooth / (2 * HALF + 1) + 1e-06
    centre_re = real_part[:, HALF : HALF + NBINS] / smooth
    centre_im = imag_part[:, HALF : HALF + NBINS] / smooth
    return jnp.stack([centre_re, centre_im], axis=1).astype(jnp.bfloat16)


def whiten(row_data):
    return normalize(jnp.dot(row_data, band_table(), preferred_element_type=jnp.float32))


def cross_parts(sources, receivers):
    src = sources.astype(jnp.float32)[:, :, None]
    rec = receivers.astype(jnp.float32)[:, None]
    real_sum = jnp.sum(src[..., 0, :] * rec[..., 0, :] + src[..., 1, :] * rec[..., 1, :], axis=0)
    imag_sum = jnp.sum(src[..., 1, :] * rec[..., 0, :] - src[..., 0, :] * rec[..., 1, :], axis=0)
    return real_sum.astype(jnp.bfloat16), imag_sum.astype(jnp.bfloat16)


SOURCE_BLOCK = 32


def lag_kernel(re_ref, im_ref, w_ref, o_ref, *, scale):
    count_rec, block, bins = re_ref.shape
    result = jnp.dot(re_ref[...].reshape(-1, bins), w_ref[:bins], preferred_element_type=jnp.float32)
    result = result + jnp.dot(im_ref[...].reshape(-1, bins), w_ref[bins:], preferred_element_type=jnp.float32)
    result = (result * scale).reshape(count_rec, block, result.shape[1])
    o_ref[...] = jnp.swapaxes(result, 0, 1)


def transform(real_part, imag_part, weights, lag_scale):
    count_src, count_rec, bins = real_part.shape
    part_spec = pl.BlockSpec((count_rec, SOURCE_BLOCK, bins), lambda i: (0, i, 0))
    return pl.pallas_call(
        functools.partial(lag_kernel, scale=lag_scale),
        out_shape=jax.ShapeDtypeStruct((count_src, count_rec, 2 * MAXLAG), jnp.float32),
        grid=(count_src // SOURCE_BLOCK,),
        in_specs=[part_spec, part_spec, pl.BlockSpec(weights.shape, lambda i: (0, 0))],
        out_specs=pl.BlockSpec((SOURCE_BLOCK, count_rec, 2 * MAXLAG), lambda i: (i, 0, 0)),
    )(jnp.swapaxes(real_part, 0, 1), jnp.swapaxes(imag_part, 0, 1), weights)


def ring_gather(value, axis_name, axis):
    size = lax.axis_size(axis_name)
    here = lax.axis_index(axis_name)
    shape = list(value.shape)
    block = shape[axis]
    shape[axis] *= size
    out = jnp.zeros(shape, value.dtype)
    for shift in range(size):
        part = value if shift == 0 else lax.ppermute(
            value, axis_name, [(i, (i + shift) % size) for i in range(size)]
        )
        start = [0] * len(shape)
        start[axis] = ((here - shift) % size) * block
        out = lax.dynamic_update_slice(out, part, start)
    return out


def collect(own):
    part = ring_gather(own, "zh", 0)
    for name in reversed(CHAN_AXES):
        part = ring_gather(part, name, 1)
    return ring_gather(part, "core", 0)


def exchange_receivers(rows):
    here = lax.axis_index(WIN_AXES)
    count = lax.axis_size(WIN_AXES)
    cores = lax.axis_size("core")
    quarter = rows.shape[0] // count
    out = jnp.zeros((count, quarter) + rows.shape[1:], rows.dtype)
    for shift in range(count):
        block = lax.dynamic_slice_in_dim(rows, ((here + shift) % count) * quarter, quarter)
        if shift:
            block = lax.ppermute(block, WIN_AXES, [(i, (i + shift) % count) for i in range(count)])
        origin = (here - shift) % count
        place = (origin % cores) * (count // cores) + origin // cores
        out = lax.dynamic_update_slice(out, block[None], (place, 0, 0, 0))
    return out


def per_device(records, source_rows):
    windows_here, rows_here, samples = records.shape
    whitened = whiten(records.reshape(windows_here * rows_here, samples)).reshape(
        windows_here, rows_here, 2, NBINS
    )
    shards = lax.axis_size(CHAN_AXES)
    block_len = source_rows.shape[1]
    per_shard = block_len // shards
    weights = lag_weights()
    lag_scale = math.sqrt(2.0 / (lax.axis_size(WIN_AXES) * windows_here * NBINS))
    receivers = exchange_receivers(whitened[0])
    shard = lax.axis_index(CHAN_AXES)
    own_rows = lax.dynamic_slice_in_dim(source_rows[0], shard * per_shard, per_shard)
    own_sources = jnp.take(whitened, own_rows, axis=1)
    sources = collect(own_sources)
    real_part, imag_part = cross_parts(sources, receivers)
    return transform(real_part, imag_part, weights, lag_scale)


def split_mesh(mesh):
    chan, win = mesh.shape["chan"], mesh.shape["win"]
    side = round(chan ** (1 / 3))
    devices = np.asarray(mesh.devices).reshape(side, side, chan // (side * side), win // 2, 2)
    return Mesh(devices, CHAN_AXES + WIN_AXES)


def solution(mesh):
    fine = split_mesh(mesh)
    in_specs = (P(WIN_AXES, CHAN_AXES, None), P())
    out_specs = P(None, CHAN_AXES + WIN_AXES, None)
    return jax.shard_map(
        per_device, mesh=fine, in_specs=in_specs, out_specs=out_specs, check_vma=False
    )
```
